32 devices in a mesh: site: 2 (over x), handler: 16 (over z, y, core).
Axes of the slice: x: 2, y: 2, z: 4, core: 2. Of those that a mesh axis runs over, the one named last changes fastest.
Arguments:
- sgt: bfloat16 [8192, 6, 2048], P(('site', 'handler')), parts along dimension 0, may hold values from -6 to 6
- taps: bfloat16 [32], replicated, may hold values from 0.019897461 to 0.099609375
- moment: float32 [6, 2048], replicated, may hold values from -2.5 to 2.5
- index: int32 [512, 32], P('handler'), may hold values from 0 to 2047
- slip: bfloat16 [512, 32, 200], P('handler'), may hold values from 0 to 0.049804688
Outputs:
- seismogram: float32 [1024, 1024], P(('site', 'handler')), parts along dimension 0
The draws below stay inside these ranges and needn't reach their ends.
There are 2 independent parts, one for each index of `site`. The reference program is written for one: setup_inputs(seed, part) draws one part's arguments, and reference() takes and returns one part's arrays. A program takes and returns all parts, laid end to end along the dimension named above; an argument that names none is the same for every part. Nothing has to cross between parts.
All inputs are finite; a program needn't handle non-finite values.
Results may differ from the reference program's by a relative error of at most 0.0014.
Values may be sent and summed in bfloat16 or wider, within the bound.
No kernel may reach another device: no remote copies, remote signals or barrier semaphores. Data moves between devices by JAX's collectives and lax.ppermute only.
A program may use at most 128 MiB of HBM per device.

```python
import jax
import jax.numpy as jnp
from jax import lax

NT = 4096
DEC = 4
TAPS = 32
L = 200
K = 32
P_SIZE = 2048
V = 512
NTD = 1024


def place_ends(entries, key, smallest, largest):
    shape = entries.shape
    place = [jax.random.randint(jax.random.fold_in(key, axis), (), 0, shape[axis]) for axis in range(len(shape))]
    entries = entries.at[tuple(place)].set(smallest)
    longest = shape.index(max(shape))
    place[longest] = (place[longest] + 1) % shape[longest]
    return entries.at[tuple(place)].set(largest)


def block_levels(own_key, dims, split, smallest, high):
    gain = 1.0
    for axis_at, parts in split:
        draws = jax.random.uniform(jax.random.fold_in(jax.random.fold_in(own_key, 6), axis_at), (parts,), jnp.float32, smallest / len(split), high / len(split))
        gain = gain * jnp.repeat(jnp.exp(draws), dims[axis_at] // parts).reshape((-1,) + (1,) * (len(dims) - 1 - axis_at))
    return gain


def noise(rng, dims, scale, bound, shards=(), dtype=jnp.bfloat16):
    drawn = jax.random.normal(rng, dims, jnp.float32) * scale
    if len(shards) > 0:
        drawn = block_levels(rng, dims, shards, -0.22, 0.18) * drawn
    return jnp.clip(drawn, min=-bound, max=bound).astype(dtype)


def setup_inputs(seed: int = 0, part: int = 0) -> dict:
    streams_of = jax.random.split(jax.random.key(seed), 6)
    part_splits = jax.random.split(jax.random.fold_in(streams_of[5], part), 6)
    sgt = noise(part_splits[0], (NT, 6, P_SIZE), 1.0, 6.0, ((0, 16),))
    taps = jnp.clip(jax.random.uniform(streams_of[1], (TAPS,), jnp.float32, 0.019897461, 0.099609375), 0.019897461, 0.099609375).astype(jnp.bfloat16)
    moment = noise(streams_of[2], (6, P_SIZE), 6 ** -0.5, 2.5, (), jnp.float32)
    index = place_ends(jax.random.randint(streams_of[3], (V, K), 0, P_SIZE), jax.random.fold_in(streams_of[3], 1), 0, P_SIZE - 1).astype(jnp.int32)
    slip = jnp.clip(0.049804688 * jax.random.uniform(streams_of[4], (V, K, L), jnp.float32) ** block_levels(streams_of[4], (V, K, L), ((0, 16),), -0.2, 0.2), 0.0, 0.049804688).astype(jnp.bfloat16)
    return {"sgt": sgt, "taps": taps, "moment": moment, "index": index, "slip": slip}


def skew_sum(spread):
    count, span, width = spread.shape
    full = width + span + 1
    padded = jnp.pad(spread, ((0, 0), (0, 0), (span, 1)))
    flat = padded.reshape(count, span * full)[:, : span * (full - 1)]
    tilted = flat.reshape(count, span, full - 1)
    return jnp.sum(tilted[:, :, span : span + width], axis=1)


def reference(sgt, taps, moment, index, slip):
    padded = jnp.pad(sgt, ((TAPS, 0), (0, 0), (0, 0)))
    filtered = jnp.zeros((NTD, 6, P_SIZE), jnp.float32)
    for which in range(TAPS):
        window = lax.slice_in_dim(padded, TAPS - which, TAPS - which + NT, DEC, 0)
        filtered = filtered + taps[which].astype(jnp.float32) * window.astype(jnp.float32)
    green = jnp.sum(moment[None, :, :] * filtered, axis=1).T.astype(jnp.bfloat16)
    block = min(32, V)
    index_groups = index.reshape(V // block, block, K)
    slip_groups = slip.reshape(V // block, block, K, L)

    def one_block(pair):
        rates, rows = pair
        picked = jnp.take(green, rows.reshape(-1), axis=0).reshape(block, K, NTD)
        spread = jnp.einsum("vkl,vkj->vlj", rates.astype(jnp.float32), picked.astype(jnp.float32))
        return skew_sum(spread)

    result = lax.map(one_block, (slip_groups, index_groups))
    return result.reshape(V, NTD)
```

```python
import jax
import jax.numpy as jnp
from jax import lax
from jax.experimental import pallas as pl
from jax.experimental.pallas import tpu as pltpu
from jax.sharding import PartitionSpec as P

DEC = 4
V_BLOCK = 8


def band_matrix(taps, rows, cols):
    row_ids = lax.broadcasted_iota(jnp.int32, (rows, cols), 0)
    col_ids = lax.broadcasted_iota(jnp.int32, (rows, cols), 1)
    lag = DEC * col_ids - row_ids
    matrix = jnp.zeros((rows, cols), jnp.bfloat16)
    for which in range(taps.shape[0]):
        matrix = jnp.where(lag == which, taps[which], matrix)
    return matrix


def conv_kernel(slip_ref, picked_ref, out_ref, spread_ref):
    vb = out_ref.shape[0]
    span = slip_ref.shape[1]
    width = out_ref.shape[1]
    col = lax.broadcasted_iota(jnp.int32, (8, width), 1)
    row = lax.broadcasted_iota(jnp.int32, (8, width), 0)
    lag = col - row

    def one(v, carry):
        spread_ref[...] = jnp.dot(slip_ref[v], picked_ref[v], preferred_element_type=jnp.float32)
        acc = jnp.zeros((8, width), jnp.float32)
        for g in range(span // 8):
            blk = spread_ref[8 * g:8 * g + 8, :]
            moved = pltpu.roll(blk, 8 * g, 1, stride=1, stride_axis=0)
            acc = acc + jnp.where(lag >= 8 * g, moved, 0.0)
        out_ref[pl.ds(v, 1), :] = jnp.sum(acc, axis=0, keepdims=True)
        return carry

    lax.fori_loop(0, vb, one, 0)


def convolve(picked, slip):
    v_local, k, width = picked.shape
    span = slip.shape[2]
    slip_t = jnp.swapaxes(slip, 1, 2)
    vb = min(V_BLOCK, v_local)
    return pl.pallas_call(
        conv_kernel,
        grid=(v_local // vb,),
        in_specs=[
            pl.BlockSpec((vb, span, k), lambda i: (i, 0, 0)),
            pl.BlockSpec((vb, k, width), lambda i: (i, 0, 0)),
        ],
        out_specs=pl.BlockSpec((vb, width), lambda i: (i, 0)),
        out_shape=jax.ShapeDtypeStruct((v_local, width), jnp.float32),
        scratch_shapes=[pltpu.VMEM((span, width), jnp.float32)],
    )(slip_t, picked)


def body(sgt, taps, moment, index, slip):
    n_handler = lax.axis_size("handler")
    me = lax.axis_index("handler")
    local_t = sgt.shape[0]
    local_j = local_t // DEC
    n_taps = taps.shape[0]
    halo = (n_taps - 1 + DEC - 1) // DEC
    lowpass = band_matrix(taps, local_t, local_j + halo)
    filtered = jnp.einsum("tj,tcp->jcp", lowpass, sgt, preferred_element_type=jnp.float32)
    partial = jnp.sum(moment[None, :, :] * filtered, axis=1)
    carried = lax.ppermute(partial[local_j:], "handler", [(i, i + 1) for i in range(n_handler - 1)])
    own = partial[:local_j]
    own = own.at[:halo].add(carried)
    green = own.astype(jnp.bfloat16).T
    piece = lax.all_gather(green, "handler", axis=1, tiled=True)
    length = piece.shape[0]
    v_local, k = index.shape
    flat_index = jnp.clip(index.reshape(-1), 0, length - 1)
    rows = jnp.take(piece, flat_index, axis=0)
    picked = rows.reshape(v_local, k, piece.shape[1])
    return convolve(picked, slip)


def solution(mesh):
    in_specs = (
        P(("site", "handler"), None, None),
        P(),
        P(),
        P("handler", None),
        P("handler", None, None),
    )
    out_specs = P(("site", "handler"), None)
    return jax.shard_map(body, mesh=mesh, in_specs=in_specs, out_specs=out_specs, check_vma=False)
```

```python
import jax
import jax.numpy as jnp
from jax import lax
from jax.experimental import pallas as pl
from jax.experimental.pallas import tpu as pltpu
from jax.sharding import Mesh, PartitionSpec as P

DEC = 4
V_BLOCK = 8


def band_matrix(taps, rows, cols):
    row_ids = lax.broadcasted_iota(jnp.int32, (rows, cols), 0)
    col_ids = lax.broadcasted_iota(jnp.int32, (rows, cols), 1)
    lag = DEC * col_ids - row_ids
    matrix = jnp.zeros((rows, cols), jnp.bfloat16)
    for which in range(taps.shape[0]):
        matrix = jnp.where(lag == which, taps[which], matrix)
    return matrix


def conv_kernel(slip_ref, picked_ref, out_ref, spread_ref):
    vb = out_ref.shape[0]
    span = slip_ref.shape[1]
    width = out_ref.shape[1]
    col = lax.broadcasted_iota(jnp.int32, (8, width), 1)
    row = lax.broadcasted_iota(jnp.int32, (8, width), 0)
    lag = col - row

    def one(v, carry):
        spread_ref[...] = jnp.dot(slip_ref[v], picked_ref[v], preferred_element_type=jnp.float32)
        acc = jnp.zeros((8, width), jnp.float32)
        for g in range(span // 8):
            blk = spread_ref[8 * g:8 * g + 8, :]
            moved = pltpu.roll(blk, 8 * g, 1, stride=1, stride_axis=0)
            acc = acc + jnp.where(lag >= 8 * g, moved, 0.0)
        out_ref[pl.ds(v, 1), :] = jnp.sum(acc, axis=0, keepdims=True)
        return carry

    lax.fori_loop(0, vb, one, 0)


def convolve(picked, slip):
    v_local, k, width = picked.shape
    span = slip.shape[2]
    slip_t = jnp.swapaxes(slip, 1, 2)
    vb = min(V_BLOCK, v_local)
    return pl.pallas_call(
        conv_kernel,
        grid=(v_local // vb,),
        in_specs=[
            pl.BlockSpec((vb, span, k), lambda i: (i, 0, 0)),
            pl.BlockSpec((vb, k, width), lambda i: (i, 0, 0)),
        ],
        out_specs=pl.BlockSpec((vb, width), lambda i: (i, 0)),
        out_shape=jax.ShapeDtypeStruct((v_local, width), jnp.float32),
        scratch_shapes=[pltpu.VMEM((span, width), jnp.float32)],
    )(slip_t, picked)


def body(sgt, taps, moment, index, slip):
    handler = ("chip", "core")
    n_handler = lax.axis_size(handler)
    local_t = sgt.shape[0]
    local_j = local_t // DEC
    n_taps = taps.shape[0]
    halo = (n_taps - 1 + DEC - 1) // DEC
    lowpass = band_matrix(taps, local_t, local_j + halo)
    filtered = jnp.einsum("tj,tcp->jcp", lowpass, sgt, preferred_element_type=jnp.float32)
    partial = jnp.sum(moment[None, :, :] * filtered, axis=1)
    carried = lax.ppermute(partial[local_j:], handler, [(i, i + 1) for i in range(n_handler - 1)])
    own = partial[:local_j]
    own = own.at[:halo].add(carried)
    green = own.astype(jnp.bfloat16)
    across = lax.all_gather(green, "chip", axis=0)
    both = lax.all_gather(across, "core", axis=1)
    piece = both.reshape(-1, both.shape[-1]).T
    length = piece.shape[0]
    v_local, k = index.shape
    flat_index = jnp.clip(index.reshape(-1), 0, length - 1)
    rows = jnp.take(piece, flat_index, axis=0)
    picked = rows.reshape(v_local, k, piece.shape[1])
    return convolve(picked, slip)


def solution(mesh):
    n_site, n_handler = mesh.devices.shape
    split = Mesh(mesh.devices.reshape(n_site, n_handler // 2, 2), ("site", "chip", "core"))
    points = ("site", "chip", "core")
    in_specs = (
        P(points, None, None),
        P(),
        P(),
        P(("chip", "core"), None),
        P(("chip", "core"), None, None),
    )
    out_specs = P(points, None)
    return jax.shard_map(body, mesh=split, in_specs=in_specs, out_specs=out_specs, check_vma=False)
```

```python
import jax
import jax.numpy as jnp
from jax import lax
from jax.experimental import pallas as pl
from jax.experimental.pallas import tpu as pltpu
from jax.sharding import PartitionSpec as P

DEC = 4
V_BLOCK = 8


def band_matrix(taps, rows, cols):
    row_ids = lax.broadcasted_iota(jnp.int32, (rows, cols), 0)
    col_ids = lax.broadcasted_iota(jnp.int32, (rows, cols), 1)
    lag = DEC * col_ids - row_ids
    matrix = jnp.zeros((rows, cols), jnp.bfloat16)
    for which in range(taps.shape[0]):
        matrix = jnp.where(lag == which, taps[which], matrix)
    return matrix


def conv_kernel(slip_ref, picked_ref, out_ref, spread_ref):
    vb = out_ref.shape[0]
    span = slip_ref.shape[1]
    width = out_ref.shape[1]
    col = lax.broadcasted_iota(jnp.int32, (8, width), 1)
    row = lax.broadcasted_iota(jnp.int32, (8, width), 0)
    lag = col - row

    def one(v, carry):
        spread_ref[...] = jnp.dot(slip_ref[v], picked_ref[v], preferred_element_type=jnp.float32)
        acc = jnp.zeros((8, width), jnp.float32)
        for g in range(span // 8):
            blk = spread_ref[8 * g:8 * g + 8, :]
            moved = pltpu.roll(blk, 8 * g, 1, stride=1, stride_axis=0)
            acc = acc + jnp.where(lag >= 8 * g, moved, 0.0)
        out_ref[pl.ds(v, 1), :] = jnp.sum(acc, axis=0, keepdims=True)
        return carry

    lax.fori_loop(0, vb, one, 0)


def convolve(picked, slip):
    v_local, k, width = picked.shape
    span = slip.shape[2]
    slip_t = jnp.swapaxes(slip, 1, 2)
    vb = min(V_BLOCK, v_local)
    return pl.pallas_call(
        conv_kernel,
        grid=(v_local // vb,),
        in_specs=[
            pl.BlockSpec((vb, span, k), lambda i: (i, 0, 0)),
            pl.BlockSpec((vb, k, width), lambda i: (i, 0, 0)),
        ],
        out_specs=pl.BlockSpec((vb, width), lambda i: (i, 0)),
        out_shape=jax.ShapeDtypeStruct((v_local, width), jnp.float32),
        scratch_shapes=[pltpu.VMEM((span, width), jnp.float32)],
    )(slip_t, picked)


def body(sgt, taps, moment, index, slip):
    n_handler = lax.axis_size("handler")
    me = lax.axis_index("handler")
    local_t = sgt.shape[0]
    local_j = local_t // DEC
    n_taps = taps.shape[0]
    halo = (n_taps - 1 + DEC - 1) // DEC
    lowpass = lax.optimization_barrier(band_matrix(taps, local_t, local_j + halo))
    by_component = jnp.transpose(sgt, (1, 0, 2))
    filtered = jnp.einsum("tj,ctp->cjp", lowpass, by_component, preferred_element_type=jnp.float32)
    partial = jnp.sum(moment[:, None, :] * filtered, axis=0)
    carried = lax.ppermute(partial[local_j:], "handler", [(i, i + 1) for i in range(n_handler - 1)])
    own = partial[:local_j]
    own = own.at[:halo].add(carried)
    green = own.astype(jnp.bfloat16).T
    piece = lax.all_gather(green, "handler", axis=1, tiled=True)
    length = piece.shape[0]
    v_local, k = index.shape
    flat_index = jnp.clip(index.reshape(-1), 0, length - 1)
    rows = jnp.take(piece, flat_index, axis=0)
    picked = rows.reshape(v_local, k, piece.shape[1])
    return convolve(picked, slip)


def solution(mesh):
    in_specs = (
        P(("site", "handler"), None, None),
        P(),
        P(),
        P("handler", None),
        P("handler", None, None),
    )
    out_specs = P(("site", "handler"), None)
    return jax.shard_map(body, mesh=mesh, in_specs=in_specs, out_specs=out_specs, check_vma=False)
```

```python
import jax
import jax.numpy as jnp
from jax import lax
from jax.experimental import pallas as pl
from jax.experimental.pallas import tpu as pltpu
from jax.sharding import PartitionSpec as P

DEC = 4
V_BLOCK = 8


def band_matrix(taps, rows, cols):
    n_taps = taps.shape[0]
    row_ids = lax.broadcasted_iota(jnp.int32, (rows, cols, n_taps), 0)
    col_ids = lax.broadcasted_iota(jnp.int32, (rows, cols, n_taps), 1)
    tap_ids = lax.broadcasted_iota(jnp.int32, (rows, cols, n_taps), 2)
    hit = DEC * col_ids - row_ids == tap_ids
    picked = jnp.where(hit, taps.astype(jnp.float32)[None, None, :], 0.0)
    return jnp.sum(picked, axis=2).astype(jnp.bfloat16)


def conv_kernel(slip_ref, picked_ref, out_ref, spread_ref):
    vb = out_ref.shape[0]
    span = slip_ref.shape[1]
    width = out_ref.shape[1]
    col = lax.broadcasted_iota(jnp.int32, (8, width), 1)
    row = lax.broadcasted_iota(jnp.int32, (8, width), 0)
    lag = col - row

    def one(v, carry):
        spread_ref[...] = jnp.dot(slip_ref[v], picked_ref[v], preferred_element_type=jnp.float32)
        acc = jnp.zeros((8, width), jnp.float32)
        for g in range(span // 8):
            blk = spread_ref[8 * g:8 * g + 8, :]
            moved = pltpu.roll(blk, 8 * g, 1, stride=1, stride_axis=0)
            acc = acc + jnp.where(lag >= 8 * g, moved, 0.0)
        out_ref[pl.ds(v, 1), :] = jnp.sum(acc, axis=0, keepdims=True)
        return carry

    lax.fori_loop(0, vb, one, 0)


def convolve(picked, slip):
    v_local, k, width = picked.shape
    span = slip.shape[2]
    slip_t = jnp.swapaxes(slip, 1, 2)
    vb = min(V_BLOCK, v_local)
    return pl.pallas_call(
        conv_kernel,
        grid=(v_local // vb,),
        in_specs=[
            pl.BlockSpec((vb, span, k), lambda i: (i, 0, 0)),
            pl.BlockSpec((vb, k, width), lambda i: (i, 0, 0)),
        ],
        out_specs=pl.BlockSpec((vb, width), lambda i: (i, 0)),
        out_shape=jax.ShapeDtypeStruct((v_local, width), jnp.float32),
        scratch_shapes=[pltpu.VMEM((span, width), jnp.float32)],
    )(slip_t, picked)


def body(sgt, taps, moment, index, slip):
    n_handler = lax.axis_size("handler")
    me = lax.axis_index("handler")
    local_t = sgt.shape[0]
    local_j = local_t // DEC
    n_taps = taps.shape[0]
    halo = (n_taps - 1 + DEC - 1) // DEC
    lowpass = lax.optimization_barrier(band_matrix(taps, local_t, local_j + halo))
    by_component = jnp.transpose(sgt, (1, 0, 2))
    filtered = jnp.einsum("tj,ctp->cjp", lowpass, by_component, preferred_element_type=jnp.float32)
    partial = jnp.sum(moment[:, None, :] * filtered, axis=0)
    carried = lax.ppermute(partial[local_j:], "handler", [(i, i + 1) for i in range(n_handler - 1)])
    own = partial[:local_j]
    own = own.at[:halo].add(carried)
    green = own.astype(jnp.bfloat16).T
    piece = lax.all_gather(green, "handler", axis=1, tiled=True)
    length = piece.shape[0]
    v_local, k = index.shape
    flat_index = jnp.clip(index.reshape(-1), 0, length - 1)
    rows = jnp.take(piece, flat_index, axis=0)
    picked = rows.reshape(v_local, k, piece.shape[1])
    return convolve(picked, slip)


def solution(mesh):
    in_specs = (
        P(("site", "handler"), None, None),
        P(),
        P(),
        P("handler", None),
        P("handler", None, None),
    )
    out_specs = P(("site", "handler"), None)
    return jax.shard_map(body, mesh=mesh, in_specs=in_specs, out_specs=out_specs, check_vma=False)
```

```python
import jax
import jax.numpy as jnp
from jax import lax
from jax.experimental import pallas as pl
from jax.experimental.pallas import tpu as pltpu
from jax.sharding import PartitionSpec as P

DEC = 4
V_BLOCK = 8


def band_matrix(taps, rows, cols):
    n_taps = taps.shape[0]
    row_ids = lax.broadcasted_iota(jnp.int32, (rows, cols, n_taps), 0)
    col_ids = lax.broadcasted_iota(jnp.int32, (rows, cols, n_taps), 1)
    tap_ids = lax.broadcasted_iota(jnp.int32, (rows, cols, n_taps), 2)
    hit = DEC * col_ids - row_ids == tap_ids
    picked = jnp.where(hit, taps.astype(jnp.float32)[None, None, :], 0.0)
    return jnp.sum(picked, axis=2).astype(jnp.bfloat16)


def conv_kernel(slip_ref, picked_ref, out_ref, spread_ref):
    vb = out_ref.shape[0]
    span = slip_ref.shape[1]
    width = out_ref.shape[1]
    col = lax.broadcasted_iota(jnp.int32, (8, width), 1)
    row = lax.broadcasted_iota(jnp.int32, (8, width), 0)
    lag = col - row

    def one(v, carry):
        spread_ref[...] = jnp.dot(slip_ref[v], picked_ref[v], preferred_element_type=jnp.float32)
        acc = jnp.zeros((8, width), jnp.float32)
        for g in range(span // 8):
            blk = spread_ref[8 * g:8 * g + 8, :]
            moved = pltpu.roll(blk, 8 * g, 1, stride=1, stride_axis=0)
            acc = acc + jnp.where(lag >= 8 * g, moved, 0.0)
        out_ref[pl.ds(v, 1), :] = jnp.sum(acc, axis=0, keepdims=True)
        return carry

    lax.fori_loop(0, vb, one, 0)


def convolve(picked, slip):
    v_local, k, width = picked.shape
    span = slip.shape[2]
    slip_t = jnp.swapaxes(slip, 1, 2)
    vb = min(V_BLOCK, v_local)
    return pl.pallas_call(
        conv_kernel,
        grid=(v_local // vb,),
        in_specs=[
            pl.BlockSpec((vb, span, k), lambda i: (i, 0, 0)),
            pl.BlockSpec((vb, k, width), lambda i: (i, 0, 0)),
        ],
        out_specs=pl.BlockSpec((vb, width), lambda i: (i, 0)),
        out_shape=jax.ShapeDtypeStruct((v_local, width), jnp.float32),
        scratch_shapes=[pltpu.VMEM((span, width), jnp.float32)],
    )(slip_t, picked)


def ring_order(devices):
    try:
        keys = [(tuple(d.coords), int(d.core_on_chip)) for d in devices]
    except AttributeError:
        return list(range(len(devices)))
    chips = sorted({c for c, _ in keys})
    dims = [a for a in range(len(chips[0])) if len({c[a] for c in chips}) > 1]
    if len(dims) == 2:
        dims.sort(key=lambda a: len({c[a] for c in chips}))
        slow, fast = dims
        lanes = sorted({c[slow] for c in chips})
        ordered = []
        for i, lane in enumerate(lanes):
            row = sorted((c for c in chips if c[slow] == lane), key=lambda c: c[fast])
            ordered += row if i % 2 == 0 else row[::-1]
        chips = ordered
    order = []
    for chip in chips:
        order += sorted((i for i, (c, _) in enumerate(keys) if c == chip), key=lambda i: keys[i][1])
    return order


def ring_gather(block, ring):
    n = len(ring)
    position = [0] * n
    for i, h in enumerate(ring):
        position[h] = i
    ring_ids = jnp.asarray(ring, jnp.int32)
    me = lax.axis_index("handler")
    mine = jnp.asarray(position, jnp.int32)[me]
    ahead = [(ring[i], ring[(i + 1) % n]) for i in range(n)]
    behind = [(ring[(i + 1) % n], ring[i]) for i in range(n)]
    n_ahead = n // 2
    n_behind = n - 1 - n_ahead
    out = jnp.zeros((n,) + block.shape, block.dtype)
    out = lax.dynamic_update_index_in_dim(out, block, me, 0)
    from_behind = block
    from_ahead = block
    for step in range(1, n_ahead + 1):
        from_behind = lax.ppermute(from_behind, "handler", ahead)
        source = ring_ids[(mine - step) % n]
        out = lax.dynamic_update_index_in_dim(out, from_behind, source, 0)
        if step <= n_behind:
            from_ahead = lax.ppermute(from_ahead, "handler", behind)
            source = ring_ids[(mine + step) % n]
            out = lax.dynamic_update_index_in_dim(out, from_ahead, source, 0)
    return out


def make_body(ring):
    def body(sgt, taps, moment, index, slip):
        n_handler = lax.axis_size("handler")
        local_t = sgt.shape[0]
        local_j = local_t // DEC
        n_taps = taps.shape[0]
        halo = (n_taps - 1 + DEC - 1) // DEC
        lowpass = lax.optimization_barrier(band_matrix(taps, local_t, local_j + halo))
        by_component = jnp.transpose(sgt, (1, 0, 2))
        filtered = jnp.einsum("tj,ctp->cjp", lowpass, by_component, preferred_element_type=jnp.float32)
        partial = jnp.sum(moment[:, None, :] * filtered, axis=0)
        carried = lax.ppermute(partial[local_j:], "handler", [(i, i + 1) for i in range(n_handler - 1)])
        own = partial[:local_j]
        own = own.at[:halo].add(carried)
        green = own.astype(jnp.bfloat16)
        stacked = ring_gather(green, ring)
        piece = stacked.reshape(-1, stacked.shape[-1]).T
        length = piece.shape[0]
        v_local, k = index.shape
        flat_index = jnp.clip(index.reshape(-1), 0, length - 1)
        rows = jnp.take(piece, flat_index, axis=0)
        picked = rows.reshape(v_local, k, piece.shape[1])
        return convolve(picked, slip)

    return body


def solution(mesh):
    ring = ring_order(list(mesh.devices[0]))
    in_specs = (
        P(("site", "handler"), None, None),
        P(),
        P(),
        P("handler", None),
        P("handler", None, None),
    )
    out_specs = P(("site", "handler"), None)
    return jax.shard_map(make_body(ring), mesh=mesh, in_specs=in_specs, out_specs=out_specs, check_vma=False)
```

```python
import jax
import jax.numpy as jnp
from jax import lax
from jax.experimental import pallas as pl
from jax.experimental.pallas import tpu as pltpu
from jax.sharding import PartitionSpec as P

DEC = 4
V_BLOCK = 8


def band_matrix(taps, rows, cols):
    n_taps = taps.shape[0]
    row_ids = lax.broadcasted_iota(jnp.int32, (rows, cols, n_taps), 0)
    col_ids = lax.broadcasted_iota(jnp.int32, (rows, cols, n_taps), 1)
    tap_ids = lax.broadcasted_iota(jnp.int32, (rows, cols, n_taps), 2)
    hit = DEC * col_ids - row_ids == tap_ids
    picked = jnp.where(hit, taps.astype(jnp.float32)[None, None, :], 0.0)
    return jnp.sum(picked, axis=2).astype(jnp.bfloat16)


def conv_kernel(slip_ref, picked_ref, out_ref, spread_ref):
    vb = out_ref.shape[0]
    span = slip_ref.shape[1]
    width = out_ref.shape[1]
    edge = min(width, -(-span // 128) * 128)
    col = lax.broadcasted_iota(jnp.int32, (8, edge), 1)
    row = lax.broadcasted_iota(jnp.int32, (8, edge), 0)
    lag = col - row

    def one(v, carry):
        spread_ref[...] = jnp.dot(slip_ref[v], picked_ref[v], preferred_element_type=jnp.float32)
        head = jnp.zeros((8, edge), jnp.float32)
        tail = jnp.zeros((8, width - edge), jnp.float32)
        for g in range(span // 8):
            blk = spread_ref[8 * g:8 * g + 8, :]
            moved = pltpu.roll(blk, 8 * g, 1, stride=1, stride_axis=0)
            head = head + jnp.where(lag >= 8 * g, moved[:, :edge], 0.0)
            tail = tail + moved[:, edge:]
        out_ref[pl.ds(v, 1), :edge] = jnp.sum(head, axis=0, keepdims=True)
        out_ref[pl.ds(v, 1), edge:] = jnp.sum(tail, axis=0, keepdims=True)
        return carry

    lax.fori_loop(0, vb, one, 0)


def convolve(picked, slip):
    v_local, k, width = picked.shape
    span = slip.shape[2]
    slip_t = jnp.swapaxes(slip, 1, 2)
    vb = min(V_BLOCK, v_local)
    return pl.pallas_call(
        conv_kernel,
        grid=(v_local // vb,),
        in_specs=[
            pl.BlockSpec((vb, span, k), lambda i: (i, 0, 0)),
            pl.BlockSpec((vb, k, width), lambda i: (i, 0, 0)),
        ],
        out_specs=pl.BlockSpec((vb, width), lambda i: (i, 0)),
        out_shape=jax.ShapeDtypeStruct((v_local, width), jnp.float32),
        scratch_shapes=[pltpu.VMEM((span, width), jnp.float32)],
    )(slip_t, picked)


def body(sgt, taps, moment, index, slip):
    n_handler = lax.axis_size("handler")
    me = lax.axis_index("handler")
    local_t = sgt.shape[0]
    local_j = local_t // DEC
    n_taps = taps.shape[0]
    halo = (n_taps - 1 + DEC - 1) // DEC
    lowpass = lax.optimization_barrier(band_matrix(taps, local_t, local_j + halo))
    by_component = jnp.transpose(sgt, (1, 0, 2))
    filtered = jnp.einsum("tj,ctp->cjp", lowpass, by_component, preferred_element_type=jnp.float32)
    partial = jnp.sum(moment[:, None, :] * filtered, axis=0)
    carried = lax.ppermute(partial[local_j:], "handler", [(i, i + 1) for i in range(n_handler - 1)])
    own = partial[:local_j]
    own = own.at[:halo].add(carried)
    green = own.astype(jnp.bfloat16).T
    piece = lax.all_gather(green, "handler", axis=1, tiled=True)
    length = piece.shape[0]
    v_local, k = index.shape
    flat_index = jnp.clip(index.reshape(-1), 0, length - 1)
    rows = jnp.take(piece, flat_index, axis=0, mode="clip")
    picked = rows.reshape(v_local, k, piece.shape[1])
    return convolve(picked, slip)


def solution(mesh):
    in_specs = (
        P(("site", "handler"), None, None),
        P(),
        P(),
        P("handler", None),
        P("handler", None, None),
    )
    out_specs = P(("site", "handler"), None)
    return jax.shard_map(body, mesh=mesh, in_specs=in_specs, out_specs=out_specs, check_vma=False)
```

```python
import jax
import jax.numpy as jnp
from jax import lax
from jax.experimental import pallas as pl
from jax.experimental.pallas import tpu as pltpu
from jax.sharding import PartitionSpec as P

DEC = 4
V_BLOCK = 8


def band_matrix(taps, rows, cols):
    n_taps = taps.shape[0]
    row_ids = lax.broadcasted_iota(jnp.int32, (rows, cols, n_taps), 0)
    col_ids = lax.broadcasted_iota(jnp.int32, (rows, cols, n_taps), 1)
    tap_ids = lax.broadcasted_iota(jnp.int32, (rows, cols, n_taps), 2)
    hit = DEC * col_ids - row_ids == tap_ids
    picked = jnp.where(hit, taps.astype(jnp.float32)[None, None, :], 0.0)
    return jnp.sum(picked, axis=2).astype(jnp.bfloat16)


SHIFTS = 8


def conv_kernel(weight_ref, picked_ref, out_ref, shifted_ref):
    vb = out_ref.shape[0]
    n_rows = weight_ref.shape[1]
    k = picked_ref.shape[1]
    width = out_ref.shape[1]
    edge = min(width, n_rows * SHIFTS)
    edge = -(-edge // 128) * 128
    col_in = lax.broadcasted_iota(jnp.int32, (k, 128), 1)
    col = lax.broadcasted_iota(jnp.int32, (8, edge), 1)
    row = lax.broadcasted_iota(jnp.int32, (8, edge), 0)
    lag = col - SHIFTS * row

    def one(v, carry):
        rows = picked_ref[v].astype(jnp.float32)
        shifted_ref[0:k, :] = rows.astype(jnp.bfloat16)
        for b in range(1, SHIFTS):
            moved = pltpu.roll(rows, b, 1)
            shifted_ref[b * k:(b + 1) * k, :128] = jnp.where(col_in >= b, moved[:, :128], 0.0).astype(jnp.bfloat16)
            shifted_ref[b * k:(b + 1) * k, 128:] = moved[:, 128:].astype(jnp.bfloat16)
        spread = jnp.dot(weight_ref[v], shifted_ref[...], preferred_element_type=jnp.float32)
        head = jnp.zeros((8, edge), jnp.float32)
        tail = jnp.zeros((8, width - edge), jnp.float32)
        for q in range(n_rows // 8):
            blk = spread[8 * q:8 * q + 8, :]
            moved = pltpu.roll(blk, 8 * SHIFTS * q, 1, stride=SHIFTS, stride_axis=0)
            head = head + jnp.where(lag >= 8 * SHIFTS * q, moved[:, :edge], 0.0)
            if width > edge:
                tail = tail + moved[:, edge:]
        out_ref[pl.ds(v, 1), :edge] = jnp.sum(head, axis=0, keepdims=True)
        if width > edge:
            out_ref[pl.ds(v, 1), edge:] = jnp.sum(tail, axis=0, keepdims=True)
        return carry

    lax.fori_loop(0, vb, one, 0)


def convolve(picked, slip):
    v_local, k, width = picked.shape
    span = slip.shape[2]
    n_rows = -(-span // SHIFTS)
    n_rows = -(-n_rows // 8) * 8
    padded = jnp.pad(slip, ((0, 0), (0, 0), (0, n_rows * SHIFTS - span)))
    weight = padded.reshape(v_local, k, n_rows, SHIFTS).transpose(0, 2, 3, 1).reshape(v_local, n_rows, SHIFTS * k)
    vb = min(V_BLOCK, v_local)
    return pl.pallas_call(
        conv_kernel,
        grid=(v_local // vb,),
        in_specs=[
            pl.BlockSpec((vb, n_rows, SHIFTS * k), lambda i: (i, 0, 0)),
            pl.BlockSpec((vb, k, width), lambda i: (i, 0, 0)),
        ],
        out_specs=pl.BlockSpec((vb, width), lambda i: (i, 0)),
        out_shape=jax.ShapeDtypeStruct((v_local, width), jnp.float32),
        scratch_shapes=[pltpu.VMEM((SHIFTS * k, width), jnp.bfloat16)],
    )(weight, picked)


def body(sgt, taps, moment, index, slip):
    n_handler = lax.axis_size("handler")
    me = lax.axis_index("handler")
    local_t = sgt.shape[0]
    local_j = local_t // DEC
    n_taps = taps.shape[0]
    halo = (n_taps - 1 + DEC - 1) // DEC
    lowpass = lax.optimization_barrier(band_matrix(taps, local_t, local_j + halo))
    by_component = jnp.transpose(sgt, (1, 0, 2))
    filtered = jnp.einsum("tj,ctp->cjp", lowpass, by_component, preferred_element_type=jnp.float32)
    partial = jnp.sum(moment[:, None, :] * filtered, axis=0)
    carried = lax.ppermute(partial[local_j:], "handler", [(i, i + 1) for i in range(n_handler - 1)])
    own = partial[:local_j]
    own = own.at[:halo].add(carried)
    green = own.astype(jnp.bfloat16).T
    piece = lax.all_gather(green, "handler", axis=1, tiled=True)
    length = piece.shape[0]
    v_local, k = index.shape
    flat_index = jnp.clip(index.reshape(-1), 0, length - 1)
    rows = jnp.take(piece, flat_index, axis=0, mode="clip")
    picked = rows.reshape(v_local, k, piece.shape[1])
    return convolve(picked, slip)


def solution(mesh):
    in_specs = (
        P(("site", "handler"), None, None),
        P(),
        P(),
        P("handler", None),
        P("handler", None, None),
    )
    out_specs = P(("site", "handler"), None)
    return jax.shard_map(body, mesh=mesh, in_specs=in_specs, out_specs=out_specs, check_vma=False)
```

```python
import jax
import jax.numpy as jnp
from jax import lax
from jax.experimental import pallas as pl
from jax.experimental.pallas import tpu as pltpu
from jax.sharding import PartitionSpec as P

DEC = 4
V_BLOCK = 8


def band_matrix(taps, rows, cols):
    n_taps = taps.shape[0]
    row_ids = lax.broadcasted_iota(jnp.int32, (rows, cols, n_taps), 0)
    col_ids = lax.broadcasted_iota(jnp.int32, (rows, cols, n_taps), 1)
    tap_ids = lax.broadcasted_iota(jnp.int32, (rows, cols, n_taps), 2)
    hit = DEC * col_ids - row_ids == tap_ids
    picked = jnp.where(hit, taps.astype(jnp.float32)[None, None, :], 0.0)
    return jnp.sum(picked, axis=2).astype(jnp.bfloat16)


SHIFTS = 4


def conv_kernel(weight_ref, picked_ref, out_ref, shifted_ref):
    vb = out_ref.shape[0]
    n_rows = weight_ref.shape[1]
    k = picked_ref.shape[1]
    width = out_ref.shape[1]
    edge = min(width, n_rows * SHIFTS)
    edge = -(-edge // 128) * 128
    col_in = lax.broadcasted_iota(jnp.int32, (k, 128), 1)
    col = lax.broadcasted_iota(jnp.int32, (8, edge), 1)
    row = lax.broadcasted_iota(jnp.int32, (8, edge), 0)
    lag = col - SHIFTS * row

    def one(v, carry):
        rows = picked_ref[v]
        shifted_ref[0:k, :] = rows
        for b in range(1, SHIFTS):
            moved = pltpu.roll(rows, b, 1)
            shifted_ref[b * k:(b + 1) * k, :128] = jnp.where(col_in >= b, moved[:, :128], jnp.zeros_like(moved[:, :128]))
            shifted_ref[b * k:(b + 1) * k, 128:] = moved[:, 128:]
        spread = jnp.dot(weight_ref[v], shifted_ref[...], preferred_element_type=jnp.float32)
        head = jnp.zeros((8, edge), jnp.float32)
        tail = jnp.zeros((8, width - edge), jnp.float32)
        for q in range(n_rows // 8):
            blk = spread[8 * q:8 * q + 8, :]
            moved = pltpu.roll(blk, 8 * SHIFTS * q, 1, stride=SHIFTS, stride_axis=0)
            head = head + jnp.where(lag >= 8 * SHIFTS * q, moved[:, :edge], 0.0)
            if width > edge:
                tail = tail + moved[:, edge:]
        out_ref[pl.ds(v, 1), :edge] = jnp.sum(head, axis=0, keepdims=True)
        if width > edge:
            out_ref[pl.ds(v, 1), edge:] = jnp.sum(tail, axis=0, keepdims=True)
        return carry

    lax.fori_loop(0, vb, one, 0)


def convolve(picked, slip):
    v_local, k, width = picked.shape
    span = slip.shape[2]
    n_rows = -(-span // SHIFTS)
    n_rows = -(-n_rows // 8) * 8
    padded = jnp.pad(slip, ((0, 0), (0, 0), (0, n_rows * SHIFTS - span)))
    weight = padded.reshape(v_local, k, n_rows, SHIFTS).transpose(0, 2, 3, 1).reshape(v_local, n_rows, SHIFTS * k)
    vb = min(V_BLOCK, v_local)
    return pl.pallas_call(
        conv_kernel,
        grid=(v_local // vb,),
        in_specs=[
            pl.BlockSpec((vb, n_rows, SHIFTS * k), lambda i: (i, 0, 0)),
            pl.BlockSpec((vb, k, width), lambda i: (i, 0, 0)),
        ],
        out_specs=pl.BlockSpec((vb, width), lambda i: (i, 0)),
        out_shape=jax.ShapeDtypeStruct((v_local, width), jnp.float32),
        scratch_shapes=[pltpu.VMEM((SHIFTS * k, width), jnp.bfloat16)],
    )(weight, picked)


def body(sgt, taps, moment, index, slip):
    n_handler = lax.axis_size("handler")
    me = lax.axis_index("handler")
    local_t = sgt.shape[0]
    local_j = local_t // DEC
    n_taps = taps.shape[0]
    halo = (n_taps - 1 + DEC - 1) // DEC
    lowpass = lax.optimization_barrier(band_matrix(taps, local_t, local_j + halo))
    by_component = jnp.transpose(sgt, (1, 0, 2))
    filtered = jnp.einsum("tj,ctp->cjp", lowpass, by_component, preferred_element_type=jnp.float32)
    partial = jnp.sum(moment[:, None, :] * filtered, axis=0)
    carried = lax.ppermute(partial[local_j:], "handler", [(i, i + 1) for i in range(n_handler - 1)])
    own = partial[:local_j]
    own = own.at[:halo].add(carried)
    green = own.astype(jnp.bfloat16).T
    piece = lax.all_gather(green, "handler", axis=1, tiled=True)
    length = piece.shape[0]
    v_local, k = index.shape
    flat_index = jnp.clip(index.reshape(-1), 0, length - 1)
    rows = jnp.take(piece, flat_index, axis=0, mode="clip")
    picked = rows.reshape(v_local, k, piece.shape[1])
    return convolve(picked, slip)


def solution(mesh):
    in_specs = (
        P(("site", "handler"), None, None),
        P(),
        P(),
        P("handler", None),
        P("handler", None, None),
    )
    out_specs = P(("site", "handler"), None)
    return jax.shard_map(body, mesh=mesh, in_specs=in_specs, out_specs=out_specs, check_vma=False)
```

```python
import jax
import jax.numpy as jnp
from jax import lax
from jax.experimental import pallas as pl
from jax.experimental.pallas import tpu as pltpu
from jax.sharding import PartitionSpec as P

DEC = 4
V_BLOCK = 8


def band_matrix(taps, rows, cols):
    n_taps = taps.shape[0]
    row_ids = lax.broadcasted_iota(jnp.int32, (rows, cols, n_taps), 0)
    col_ids = lax.broadcasted_iota(jnp.int32, (rows, cols, n_taps), 1)
    tap_ids = lax.broadcasted_iota(jnp.int32, (rows, cols, n_taps), 2)
    hit = DEC * col_ids - row_ids == tap_ids
    picked = jnp.where(hit, taps.astype(jnp.float32)[None, None, :], 0.0)
    return jnp.sum(picked, axis=2).astype(jnp.bfloat16)


SHIFTS = 4


def conv_kernel(weight_ref, picked_ref, out_ref, shifted_ref):
    vb = out_ref.shape[0]
    n_rows = weight_ref.shape[1]
    k = picked_ref.shape[1]
    width = out_ref.shape[1]
    edge = min(width, n_rows * SHIFTS)
    edge = -(-edge // 128) * 128
    col_in = lax.broadcasted_iota(jnp.int32, (k, 128), 1)
    col = lax.broadcasted_iota(jnp.int32, (8, edge), 1)
    row = lax.broadcasted_iota(jnp.int32, (8, edge), 0)
    lag = col - SHIFTS * row

    def one(v, carry):
        rows = picked_ref[v]
        shifted_ref[0:k, :] = rows
        for b in range(1, SHIFTS):
            moved = pltpu.roll(rows, b, 1)
            shifted_ref[b * k:(b + 1) * k, :128] = jnp.where(col_in >= b, moved[:, :128], jnp.zeros_like(moved[:, :128]))
            shifted_ref[b * k:(b + 1) * k, 128:] = moved[:, 128:]
        spread = jnp.dot(weight_ref[v], shifted_ref[...], preferred_element_type=jnp.float32)
        head = jnp.zeros((8, edge), jnp.float32)
        tail = jnp.zeros((8, width - edge), jnp.float32)
        for q in range(n_rows // 8):
            blk = spread[8 * q:8 * q + 8, :]
            moved = pltpu.roll(blk, 8 * SHIFTS * q, 1, stride=SHIFTS, stride_axis=0)
            head = head + jnp.where(lag >= 8 * SHIFTS * q, moved[:, :edge], 0.0)
            if width > edge:
                tail = tail + moved[:, edge:]
        out_ref[pl.ds(v, 1), :edge] = jnp.sum(head, axis=0, keepdims=True)
        if width > edge:
            out_ref[pl.ds(v, 1), edge:] = jnp.sum(tail, axis=0, keepdims=True)
        return carry

    lax.fori_loop(0, vb, one, 0)


def convolve(picked, slip):
    v_local, k, width = picked.shape
    span = slip.shape[2]
    n_rows = -(-span // SHIFTS)
    n_rows = -(-n_rows // 8) * 8
    padded = jnp.pad(slip, ((0, 0), (0, 0), (0, n_rows * SHIFTS - span)))
    weight = padded.reshape(v_local, k, n_rows, SHIFTS).transpose(0, 2, 3, 1).reshape(v_local, n_rows, SHIFTS * k)
    vb = min(V_BLOCK, v_local)
    return pl.pallas_call(
        conv_kernel,
        grid=(v_local // vb,),
        in_specs=[
            pl.BlockSpec((vb, n_rows, SHIFTS * k), lambda i: (i, 0, 0)),
            pl.BlockSpec((vb, k, width), lambda i: (i, 0, 0)),
        ],
        out_specs=pl.BlockSpec((vb, width), lambda i: (i, 0)),
        out_shape=jax.ShapeDtypeStruct((v_local, width), jnp.float32),
        scratch_shapes=[pltpu.VMEM((SHIFTS * k, width), jnp.bfloat16)],
    )(weight, picked)


def body(sgt, taps, moment, index, slip):
    n_handler = lax.axis_size("handler")
    me = lax.axis_index("handler")
    local_t = sgt.shape[0]
    local_j = local_t // DEC
    n_taps = taps.shape[0]
    halo = (n_taps - 1 + DEC - 1) // DEC
    lowpass = lax.optimization_barrier(band_matrix(taps, local_t, local_j + halo))
    by_component = jnp.transpose(sgt, (1, 0, 2))
    filtered = jnp.einsum("tj,ctp->cjp", lowpass, by_component, preferred_element_type=jnp.float32)
    partial = jnp.sum(moment[:, None, :] * filtered, axis=0)
    carried = lax.ppermute(partial[local_j:], "handler", [(i, i + 1) for i in range(n_handler - 1)])
    own = partial[:local_j]
    own = own.at[:halo].add(carried)
    by_time = lax.all_gather(own.astype(jnp.bfloat16), "handler", axis=0, tiled=True)
    length = by_time.shape[1]
    v_local, k = index.shape
    flat_index = jnp.clip(index.reshape(-1), 0, length - 1)
    choose = (flat_index[:, None] == lax.broadcasted_iota(jnp.int32, (flat_index.shape[0], length), 1))
    rows = jnp.einsum("np,jp->nj", choose.astype(jnp.bfloat16), by_time, preferred_element_type=jnp.float32)
    picked = rows.astype(jnp.bfloat16).reshape(v_local, k, by_time.shape[0])
    return convolve(picked, slip)


def solution(mesh):
    in_specs = (
        P(("site", "handler"), None, None),
        P(),
        P(),
        P("handler", None),
        P("handler", None, None),
    )
    out_specs = P(("site", "handler"), None)
    return jax.shard_map(body, mesh=mesh, in_specs=in_specs, out_specs=out_specs, check_vma=False)
```

```python
import jax
import jax.numpy as jnp
from jax import lax
from jax.experimental import pallas as pl
from jax.experimental.pallas import tpu as pltpu
from jax.sharding import PartitionSpec as P

DEC = 4
V_BLOCK = 8


def band_matrix(taps, rows, cols):
    n_taps = taps.shape[0]
    row_ids = lax.broadcasted_iota(jnp.int32, (rows, cols, n_taps), 0)
    col_ids = lax.broadcasted_iota(jnp.int32, (rows, cols, n_taps), 1)
    tap_ids = lax.broadcasted_iota(jnp.int32, (rows, cols, n_taps), 2)
    hit = DEC * col_ids - row_ids == tap_ids
    picked = jnp.where(hit, taps.astype(jnp.float32)[None, None, :], 0.0)
    return jnp.sum(picked, axis=2).astype(jnp.bfloat16)


SHIFTS = 4


def conv_kernel(weight_ref, picked_ref, out_ref, shifted_ref):
    vb = out_ref.shape[0]
    n_rows = weight_ref.shape[1]
    k = picked_ref.shape[1]
    width = out_ref.shape[1]
    edge = min(width, n_rows * SHIFTS)
    edge = -(-edge // 128) * 128
    col_in = lax.broadcasted_iota(jnp.int32, (k, 128), 1)
    col = lax.broadcasted_iota(jnp.int32, (8, edge), 1)
    row = lax.broadcasted_iota(jnp.int32, (8, edge), 0)
    lag = col - SHIFTS * row

    def one(v, carry):
        rows = picked_ref[v]
        shifted_ref[0:k, :] = rows
        for b in range(1, SHIFTS):
            moved = pltpu.roll(rows, b, 1)
            shifted_ref[b * k:(b + 1) * k, :128] = jnp.where(col_in >= b, moved[:, :128], jnp.zeros_like(moved[:, :128]))
            shifted_ref[b * k:(b + 1) * k, 128:] = moved[:, 128:]
        spread = jnp.dot(weight_ref[v], shifted_ref[...], preferred_element_type=jnp.float32)
        head = jnp.zeros((8, edge), jnp.float32)
        tail = jnp.zeros((8, width - edge), jnp.float32)
        for q in range(n_rows // 8):
            blk = spread[8 * q:8 * q + 8, :]
            moved = pltpu.roll(blk, 8 * SHIFTS * q, 1, stride=SHIFTS, stride_axis=0)
            head = head + jnp.where(lag >= 8 * SHIFTS * q, moved[:, :edge], 0.0)
            if width > edge:
                tail = tail + moved[:, edge:]
        out_ref[pl.ds(v, 1), :edge] = jnp.sum(head, axis=0, keepdims=True)
        if width > edge:
            out_ref[pl.ds(v, 1), edge:] = jnp.sum(tail, axis=0, keepdims=True)
        return carry

    lax.fori_loop(0, vb, one, 0)


def convolve(picked, slip):
    v_local, k, width = picked.shape
    span = slip.shape[2]
    n_rows = -(-span // SHIFTS)
    n_rows = -(-n_rows // 8) * 8
    padded = jnp.pad(slip, ((0, 0), (0, 0), (0, n_rows * SHIFTS - span)))
    weight = padded.reshape(v_local, k, n_rows, SHIFTS).transpose(0, 2, 3, 1).reshape(v_local, n_rows, SHIFTS * k)
    vb = min(V_BLOCK, v_local)
    return pl.pallas_call(
        conv_kernel,
        grid=(v_local // vb,),
        in_specs=[
            pl.BlockSpec((vb, n_rows, SHIFTS * k), lambda i: (i, 0, 0)),
            pl.BlockSpec((vb, k, width), lambda i: (i, 0, 0)),
        ],
        out_specs=pl.BlockSpec((vb, width), lambda i: (i, 0)),
        out_shape=jax.ShapeDtypeStruct((v_local, width), jnp.float32),
        scratch_shapes=[pltpu.VMEM((SHIFTS * k, width), jnp.bfloat16)],
    )(weight, picked)


N_CHUNKS = 2


def body(sgt, taps, moment, index, slip):
    n_handler = lax.axis_size("handler")
    local_t = sgt.shape[0]
    local_j = local_t // DEC
    n_taps = taps.shape[0]
    halo = (n_taps - 1 + DEC - 1) // DEC
    length = sgt.shape[2]
    width = length // N_CHUNKS
    v_local, k = index.shape
    flat_index = jnp.clip(index.reshape(-1), 0, length - 1)
    lowpass = lax.optimization_barrier(band_matrix(taps, local_t, local_j + halo))
    by_component = jnp.transpose(sgt, (1, 0, 2))
    rows = None
    for chunk in range(N_CHUNKS):
        cols = slice(chunk * width, (chunk + 1) * width)
        filtered = jnp.einsum("tj,ctp->cjp", lowpass, by_component[:, :, cols], preferred_element_type=jnp.float32)
        partial = jnp.sum(moment[:, None, cols] * filtered, axis=0)
        carried = lax.ppermute(partial[local_j:], "handler", [(i, i + 1) for i in range(n_handler - 1)])
        own = partial[:local_j]
        own = own.at[:halo].add(carried)
        by_time = lax.all_gather(own.astype(jnp.bfloat16), "handler", axis=0, tiled=True)
        point_ids = chunk * width + lax.broadcasted_iota(jnp.int32, (flat_index.shape[0], width), 1)
        choose = (flat_index[:, None] == point_ids).astype(jnp.bfloat16)
        part = jnp.einsum("np,jp->nj", choose, by_time, preferred_element_type=jnp.float32)
        rows = part if rows is None else rows + part
    picked = rows.astype(jnp.bfloat16).reshape(v_local, k, rows.shape[1])
    return convolve(picked, slip)


def solution(mesh):
    in_specs = (
        P(("site", "handler"), None, None),
        P(),
        P(),
        P("handler", None),
        P("handler", None, None),
    )
    out_specs = P(("site", "handler"), None)
    return jax.shard_map(body, mesh=mesh, in_specs=in_specs, out_specs=out_specs, check_vma=False)
```

```python
import jax
import jax.numpy as jnp
from jax import lax
from jax.experimental import pallas as pl
from jax.experimental.pallas import tpu as pltpu
from jax.sharding import PartitionSpec as P

DEC = 4
V_BLOCK = 8


def band_matrix(taps, rows, cols):
    n_taps = taps.shape[0]
    row_ids = lax.broadcasted_iota(jnp.int32, (rows, cols, n_taps), 0)
    col_ids = lax.broadcasted_iota(jnp.int32, (rows, cols, n_taps), 1)
    tap_ids = lax.broadcasted_iota(jnp.int32, (rows, cols, n_taps), 2)
    hit = DEC * col_ids - row_ids == tap_ids
    picked = jnp.where(hit, taps.astype(jnp.float32)[None, None, :], 0.0)
    return jnp.sum(picked, axis=2).astype(jnp.bfloat16)


SHIFTS = 2


def conv_kernel(weight_ref, picked_ref, out_ref, shifted_ref):
    vb = out_ref.shape[0]
    n_rows = weight_ref.shape[1]
    k = picked_ref.shape[1]
    width = out_ref.shape[1]
    edge = min(width, n_rows * SHIFTS)
    edge = -(-edge // 128) * 128
    col_in = lax.broadcasted_iota(jnp.int32, (k, 128), 1)
    col = lax.broadcasted_iota(jnp.int32, (8, edge), 1)
    row = lax.broadcasted_iota(jnp.int32, (8, edge), 0)
    lag = col - SHIFTS * row

    def one(v, carry):
        rows = picked_ref[v]
        shifted_ref[0:k, :] = rows
        for b in range(1, SHIFTS):
            moved = pltpu.roll(rows, b, 1)
            shifted_ref[b * k:(b + 1) * k, :128] = jnp.where(col_in >= b, moved[:, :128], jnp.zeros_like(moved[:, :128]))
            shifted_ref[b * k:(b + 1) * k, 128:] = moved[:, 128:]
        spread = jnp.dot(weight_ref[v], shifted_ref[...], preferred_element_type=jnp.float32)
        head = jnp.zeros((8, edge), jnp.float32)
        tail = jnp.zeros((8, width - edge), jnp.float32)
        for q in range(n_rows // 8):
            blk = spread[8 * q:8 * q + 8, :]
            moved = pltpu.roll(blk, 8 * SHIFTS * q, 1, stride=SHIFTS, stride_axis=0)
            head = head + jnp.where(lag >= 8 * SHIFTS * q, moved[:, :edge], 0.0)
            if width > edge:
                tail = tail + moved[:, edge:]
        out_ref[pl.ds(v, 1), :edge] = jnp.sum(head, axis=0, keepdims=True)
        if width > edge:
            out_ref[pl.ds(v, 1), edge:] = jnp.sum(tail, axis=0, keepdims=True)
        return carry

    lax.fori_loop(0, vb, one, 0)


def convolve(picked, slip):
    v_local, k, width = picked.shape
    span = slip.shape[2]
    n_rows = -(-span // SHIFTS)
    n_rows = -(-n_rows // 8) * 8
    padded = jnp.pad(slip, ((0, 0), (0, 0), (0, n_rows * SHIFTS - span)))
    weight = padded.reshape(v_local, k, n_rows, SHIFTS).transpose(0, 2, 3, 1).reshape(v_local, n_rows, SHIFTS * k)
    vb = min(V_BLOCK, v_local)
    return pl.pallas_call(
        conv_kernel,
        grid=(v_local // vb,),
        in_specs=[
            pl.BlockSpec((vb, n_rows, SHIFTS * k), lambda i: (i, 0, 0)),
            pl.BlockSpec((vb, k, width), lambda i: (i, 0, 0)),
        ],
        out_specs=pl.BlockSpec((vb, width), lambda i: (i, 0)),
        out_shape=jax.ShapeDtypeStruct((v_local, width), jnp.float32),
        scratch_shapes=[pltpu.VMEM((SHIFTS * k, width), jnp.bfloat16)],
    )(weight, picked)


def body(sgt, taps, moment, index, slip):
    n_handler = lax.axis_size("handler")
    me = lax.axis_index("handler")
    local_t = sgt.shape[0]
    local_j = local_t // DEC
    n_taps = taps.shape[0]
    halo = (n_taps - 1 + DEC - 1) // DEC
    lowpass = lax.optimization_barrier(band_matrix(taps, local_t, local_j + halo))
    by_component = jnp.transpose(sgt, (1, 0, 2))
    tail = jnp.einsum("tj,ctp->cjp", lowpass[local_t - n_taps:, local_j:], by_component[:, local_t - n_taps:, :],
                      preferred_element_type=jnp.float32)
    carried = lax.ppermute(jnp.sum(moment[:, None, :] * tail, axis=0), "handler",
                           [(i, i + 1) for i in range(n_handler - 1)])
    filtered = jnp.einsum("tj,ctp->cjp", lowpass[:, :local_j], by_component, preferred_element_type=jnp.float32)
    own = jnp.sum(moment[:, None, :] * filtered, axis=0)
    own = own.at[:halo].add(carried)
    by_time = lax.all_gather(own.astype(jnp.bfloat16), "handler", axis=0, tiled=True)
    length = by_time.shape[1]
    v_local, k = index.shape
    flat_index = jnp.clip(index.reshape(-1), 0, length - 1)
    choose = (flat_index[:, None] == lax.broadcasted_iota(jnp.int32, (flat_index.shape[0], length), 1))
    rows = jnp.einsum("np,jp->nj", choose.astype(jnp.bfloat16), by_time, preferred_element_type=jnp.float32)
    picked = rows.astype(jnp.bfloat16).reshape(v_local, k, by_time.shape[0])
    return convolve(picked, slip)


def solution(mesh):
    in_specs = (
        P(("site", "handler"), None, None),
        P(),
        P(),
        P("handler", None),
        P("handler", None, None),
    )
    out_specs = P(("site", "handler"), None)
    return jax.shard_map(body, mesh=mesh, in_specs=in_specs, out_specs=out_specs, check_vma=False)
```

```python
import jax
import jax.numpy as jnp
from jax import lax
from jax.experimental import pallas as pl
from jax.experimental.pallas import tpu as pltpu
from jax.sharding import PartitionSpec as P

DEC = 4
V_BLOCK = 8


def band_matrix(taps, rows, cols):
    n_taps = taps.shape[0]
    row_ids = lax.broadcasted_iota(jnp.int32, (rows, cols, n_taps), 0)
    col_ids = lax.broadcasted_iota(jnp.int32, (rows, cols, n_taps), 1)
    tap_ids = lax.broadcasted_iota(jnp.int32, (rows, cols, n_taps), 2)
    hit = DEC * col_ids - row_ids == tap_ids
    picked = jnp.where(hit, taps.astype(jnp.float32)[None, None, :], 0.0)
    return jnp.sum(picked, axis=2).astype(jnp.bfloat16)


SHIFTS = 4


def conv_kernel(weight_ref, picked_ref, out_ref, shifted_ref):
    vb = out_ref.shape[0]
    n_rows = weight_ref.shape[1]
    k = picked_ref.shape[1]
    width = out_ref.shape[1]
    edge = min(width, n_rows * SHIFTS)
    edge = -(-edge // 128) * 128
    col_in = lax.broadcasted_iota(jnp.int32, (k, 128), 1)
    col = lax.broadcasted_iota(jnp.int32, (8, edge), 1)
    row = lax.broadcasted_iota(jnp.int32, (8, edge), 0)
    lag = col - SHIFTS * row

    def one(v, carry):
        rows = picked_ref[v]
        shifted_ref[0:k, :] = rows
        for b in range(1, SHIFTS):
            moved = pltpu.roll(rows, b, 1)
            shifted_ref[b * k:(b + 1) * k, :128] = jnp.where(col_in >= b, moved[:, :128], jnp.zeros_like(moved[:, :128]))
            shifted_ref[b * k:(b + 1) * k, 128:] = moved[:, 128:]
        spread = jnp.dot(weight_ref[v], shifted_ref[...], preferred_element_type=jnp.float32)
        head = jnp.zeros((8, edge), jnp.float32)
        tail = jnp.zeros((8, width - edge), jnp.float32)
        for q in range(n_rows // 8):
            blk = spread[8 * q:8 * q + 8, :]
            moved = pltpu.roll(blk, 8 * SHIFTS * q, 1, stride=SHIFTS, stride_axis=0)
            head = head + jnp.where(lag >= 8 * SHIFTS * q, moved[:, :edge], 0.0)
            if width > edge:
                tail = tail + moved[:, edge:]
        out_ref[pl.ds(v, 1), :edge] = jnp.sum(head, axis=0, keepdims=True)
        if width > edge:
            out_ref[pl.ds(v, 1), edge:] = jnp.sum(tail, axis=0, keepdims=True)
        return carry

    lax.fori_loop(0, vb, one, 0)


def convolve(picked, slip):
    v_local, k, width = picked.shape
    span = slip.shape[2]
    n_rows = -(-span // SHIFTS)
    n_rows = -(-n_rows // 8) * 8
    padded = jnp.pad(slip, ((0, 0), (0, 0), (0, n_rows * SHIFTS - span)))
    weight = padded.reshape(v_local, k, n_rows, SHIFTS).transpose(0, 2, 3, 1).reshape(v_local, n_rows, SHIFTS * k)
    vb = min(V_BLOCK, v_local)
    return pl.pallas_call(
        conv_kernel,
        grid=(v_local // vb,),
        in_specs=[
            pl.BlockSpec((vb, n_rows, SHIFTS * k), lambda i: (i, 0, 0)),
            pl.BlockSpec((vb, k, width), lambda i: (i, 0, 0)),
        ],
        out_specs=pl.BlockSpec((vb, width), lambda i: (i, 0)),
        out_shape=jax.ShapeDtypeStruct((v_local, width), jnp.float32),
        scratch_shapes=[pltpu.VMEM((SHIFTS * k, width), jnp.bfloat16)],
    )(weight, picked)


def body(sgt, taps, moment, index, slip):
    n_handler = lax.axis_size("handler")
    me = lax.axis_index("handler")
    local_t = sgt.shape[0]
    local_j = local_t // DEC
    n_taps = taps.shape[0]
    halo = (n_taps - 1 + DEC - 1) // DEC
    lowpass = lax.optimization_barrier(band_matrix(taps, local_t, local_j + halo))
    by_component = jnp.transpose(sgt, (1, 0, 2))
    tail = jnp.einsum("tj,ctp->cjp", lowpass[local_t - n_taps:, local_j:], by_component[:, local_t - n_taps:, :],
                      preferred_element_type=jnp.float32)
    carried = lax.ppermute(jnp.sum(moment[:, None, :] * tail, axis=0), "handler",
                           [(i, i + 1) for i in range(n_handler - 1)])
    filtered = jnp.einsum("tj,ctp->cjp", lowpass[:, :local_j], by_component, preferred_element_type=jnp.float32)
    own = jnp.sum(moment[:, None, :] * filtered, axis=0)
    own = own.at[:halo].add(carried)
    by_time = lax.all_gather(own.astype(jnp.bfloat16), "handler", axis=0, tiled=True)
    length = by_time.shape[1]
    v_local, k = index.shape
    flat_index = jnp.clip(index.reshape(-1), 0, length - 1)
    choose = (flat_index[:, None] == lax.broadcasted_iota(jnp.int32, (flat_index.shape[0], length), 1))
    rows = jnp.einsum("np,jp->nj", choose.astype(jnp.bfloat16), by_time, preferred_element_type=jnp.float32)
    picked = rows.astype(jnp.bfloat16).reshape(v_local, k, by_time.shape[0])
    return convolve(picked, slip)


def solution(mesh):
    in_specs = (
        P(("site", "handler"), None, None),
        P(),
        P(),
        P("handler", None),
        P("handler", None, None),
    )
    out_specs = P(("site", "handler"), None)
    return jax.shard_map(body, mesh=mesh, in_specs=in_specs, out_specs=out_specs, check_vma=False)
```

```python
import jax
import jax.numpy as jnp
from jax import lax
from jax.experimental import pallas as pl
from jax.experimental.pallas import tpu as pltpu
from jax.sharding import PartitionSpec as P

DEC = 4
V_BLOCK = 8


def band_matrix(taps, rows, cols):
    n_taps = taps.shape[0]
    row_ids = lax.broadcasted_iota(jnp.int32, (rows, cols, n_taps), 0)
    col_ids = lax.broadcasted_iota(jnp.int32, (rows, cols, n_taps), 1)
    tap_ids = lax.broadcasted_iota(jnp.int32, (rows, cols, n_taps), 2)
    hit = DEC * col_ids - row_ids == tap_ids
    picked = jnp.where(hit, taps.astype(jnp.float32)[None, None, :], 0.0)
    return jnp.sum(picked, axis=2).astype(jnp.bfloat16)


SHIFTS = 4


def conv_kernel(weight_ref, picked_ref, out_ref, shifted_ref):
    vb = out_ref.shape[0]
    n_rows = weight_ref.shape[1]
    k = picked_ref.shape[1]
    width = out_ref.shape[1]
    edge = min(width, n_rows * SHIFTS)
    edge = -(-edge // 128) * 128
    col_in = lax.broadcasted_iota(jnp.int32, (k, 128), 1)
    col = lax.broadcasted_iota(jnp.int32, (8, edge), 1)
    row = lax.broadcasted_iota(jnp.int32, (8, edge), 0)
    lag = col - SHIFTS * row

    for v in range(vb):
        slot = v % 2
        rows = picked_ref[v]
        shifted_ref[slot, 0:k, :] = rows
        for b in range(1, SHIFTS):
            moved = pltpu.roll(rows, b, 1)
            shifted_ref[slot, b * k:(b + 1) * k, :128] = jnp.where(col_in >= b, moved[:, :128], jnp.zeros_like(moved[:, :128]))
            shifted_ref[slot, b * k:(b + 1) * k, 128:] = moved[:, 128:]
        spread = jnp.dot(weight_ref[v], shifted_ref[slot], preferred_element_type=jnp.float32)
        head = jnp.zeros((8, edge), jnp.float32)
        tail = jnp.zeros((8, width - edge), jnp.float32)
        for q in range(n_rows // 8):
            blk = spread[8 * q:8 * q + 8, :]
            moved = pltpu.roll(blk, 8 * SHIFTS * q, 1, stride=SHIFTS, stride_axis=0)
            head = head + jnp.where(lag >= 8 * SHIFTS * q, moved[:, :edge], 0.0)
            if width > edge:
                tail = tail + moved[:, edge:]
        out_ref[v:v + 1, :edge] = jnp.sum(head, axis=0, keepdims=True)
        if width > edge:
            out_ref[v:v + 1, edge:] = jnp.sum(tail, axis=0, keepdims=True)


def convolve(picked, slip):
    v_local, k, width = picked.shape
    span = slip.shape[2]
    n_rows = -(-span // SHIFTS)
    n_rows = -(-n_rows // 8) * 8
    padded = jnp.pad(slip, ((0, 0), (0, 0), (0, n_rows * SHIFTS - span)))
    weight = padded.reshape(v_local, k, n_rows, SHIFTS).transpose(0, 2, 3, 1).reshape(v_local, n_rows, SHIFTS * k)
    vb = min(V_BLOCK, v_local)
    return pl.pallas_call(
        conv_kernel,
        grid=(v_local // vb,),
        in_specs=[
            pl.BlockSpec((vb, n_rows, SHIFTS * k), lambda i: (i, 0, 0)),
            pl.BlockSpec((vb, k, width), lambda i: (i, 0, 0)),
        ],
        out_specs=pl.BlockSpec((vb, width), lambda i: (i, 0)),
        out_shape=jax.ShapeDtypeStruct((v_local, width), jnp.float32),
        scratch_shapes=[pltpu.VMEM((2, SHIFTS * k, width), jnp.bfloat16)],
    )(weight, picked)


def body(sgt, taps, moment, index, slip):
    n_handler = lax.axis_size("handler")
    me = lax.axis_index("handler")
    local_t = sgt.shape[0]
    local_j = local_t // DEC
    n_taps = taps.shape[0]
    halo = (n_taps - 1 + DEC - 1) // DEC
    lowpass = lax.optimization_barrier(band_matrix(taps, local_t, local_j + halo))
    by_component = jnp.transpose(sgt, (1, 0, 2))
    tail = jnp.einsum("tj,ctp->cjp", lowpass[local_t - n_taps:, local_j:], by_component[:, local_t - n_taps:, :],
                      preferred_element_type=jnp.float32)
    carried = lax.ppermute(jnp.sum(moment[:, None, :] * tail, axis=0), "handler",
                           [(i, i + 1) for i in range(n_handler - 1)])
    filtered = jnp.einsum("tj,ctp->cjp", lowpass[:, :local_j], by_component, preferred_element_type=jnp.float32)
    own = jnp.sum(moment[:, None, :] * filtered, axis=0)
    own = own.at[:halo].add(carried)
    by_time = lax.all_gather(own.astype(jnp.bfloat16), "handler", axis=0, tiled=True)
    length = by_time.shape[1]
    v_local, k = index.shape
    flat_index = jnp.clip(index.reshape(-1), 0, length - 1)
    choose = (flat_index[:, None] == lax.broadcasted_iota(jnp.int32, (flat_index.shape[0], length), 1))
    rows = jnp.einsum("np,jp->nj", choose.astype(jnp.bfloat16), by_time, preferred_element_type=jnp.float32)
    picked = rows.astype(jnp.bfloat16).reshape(v_local, k, by_time.shape[0])
    return convolve(picked, slip)


def solution(mesh):
    in_specs = (
        P(("site", "handler"), None, None),
        P(),
        P(),
        P("handler", None),
        P("handler", None, None),
    )
    out_specs = P(("site", "handler"), None)
    return jax.shard_map(body, mesh=mesh, in_specs=in_specs, out_specs=out_specs, check_vma=False)
```

```python
import jax
import jax.numpy as jnp
from jax import lax
from jax.experimental import pallas as pl
from jax.experimental.pallas import tpu as pltpu
from jax.sharding import PartitionSpec as P

DEC = 4
V_BLOCK = 8


def band_matrix(taps, rows, cols):
    n_taps = taps.shape[0]
    row_ids = lax.broadcasted_iota(jnp.int32, (rows, cols, n_taps), 0)
    col_ids = lax.broadcasted_iota(jnp.int32, (rows, cols, n_taps), 1)
    tap_ids = lax.broadcasted_iota(jnp.int32, (rows, cols, n_taps), 2)
    hit = DEC * col_ids - row_ids == tap_ids
    picked = jnp.where(hit, taps.astype(jnp.float32)[None, None, :], 0.0)
    return jnp.sum(picked, axis=2).astype(jnp.bfloat16)


SHIFTS = 2


def conv_kernel(weight_ref, picked_ref, out_ref, shifted_ref):
    vb = out_ref.shape[0]
    n_rows = weight_ref.shape[1]
    k = picked_ref.shape[1]
    width = out_ref.shape[1]
    edge = min(width, n_rows * SHIFTS)
    edge = -(-edge // 128) * 128
    col_in = lax.broadcasted_iota(jnp.int32, (k, 128), 1)
    col = lax.broadcasted_iota(jnp.int32, (8, edge), 1)
    row = lax.broadcasted_iota(jnp.int32, (8, edge), 0)
    lag = col - SHIFTS * row

    for v in range(vb):
        slot = v % 2
        rows = picked_ref[v]
        shifted_ref[slot, 0:k, :] = rows
        for b in range(1, SHIFTS):
            moved = pltpu.roll(rows, b, 1)
            shifted_ref[slot, b * k:(b + 1) * k, :128] = jnp.where(col_in >= b, moved[:, :128], jnp.zeros_like(moved[:, :128]))
            shifted_ref[slot, b * k:(b + 1) * k, 128:] = moved[:, 128:]
        spread = jnp.dot(weight_ref[v], shifted_ref[slot], preferred_element_type=jnp.float32)
        head = jnp.zeros((8, edge), jnp.float32)
        tail = jnp.zeros((8, width - edge), jnp.float32)
        for q in range(n_rows // 8):
            blk = spread[8 * q:8 * q + 8, :]
            moved = pltpu.roll(blk, 8 * SHIFTS * q, 1, stride=SHIFTS, stride_axis=0)
            head = head + jnp.where(lag >= 8 * SHIFTS * q, moved[:, :edge], 0.0)
            if width > edge:
                tail = tail + moved[:, edge:]
        out_ref[v:v + 1, :edge] = jnp.sum(head, axis=0, keepdims=True)
        if width > edge:
            out_ref[v:v + 1, edge:] = jnp.sum(tail, axis=0, keepdims=True)


def convolve(picked, slip):
    v_local, k, width = picked.shape
    span = slip.shape[2]
    n_rows = -(-span // SHIFTS)
    n_rows = -(-n_rows // 8) * 8
    padded = jnp.pad(slip, ((0, 0), (0, 0), (0, n_rows * SHIFTS - span)))
    weight = padded.reshape(v_local, k, n_rows, SHIFTS).transpose(0, 2, 3, 1).reshape(v_local, n_rows, SHIFTS * k)
    vb = min(V_BLOCK, v_local)
    return pl.pallas_call(
        conv_kernel,
        grid=(v_local // vb,),
        in_specs=[
            pl.BlockSpec((vb, n_rows, SHIFTS * k), lambda i: (i, 0, 0)),
            pl.BlockSpec((vb, k, width), lambda i: (i, 0, 0)),
        ],
        out_specs=pl.BlockSpec((vb, width), lambda i: (i, 0)),
        out_shape=jax.ShapeDtypeStruct((v_local, width), jnp.float32),
        scratch_shapes=[pltpu.VMEM((2, SHIFTS * k, width), jnp.bfloat16)],
    )(weight, picked)


def body(sgt, taps, moment, index, slip):
    n_handler = lax.axis_size("handler")
    me = lax.axis_index("handler")
    local_t = sgt.shape[0]
    local_j = local_t // DEC
    n_taps = taps.shape[0]
    halo = (n_taps - 1 + DEC - 1) // DEC
    lowpass = lax.optimization_barrier(band_matrix(taps, local_t, local_j + halo))
    by_component = jnp.transpose(sgt, (1, 0, 2))
    tail = jnp.einsum("tj,ctp->cjp", lowpass[local_t - n_taps:, local_j:], by_component[:, local_t - n_taps:, :],
                      preferred_element_type=jnp.float32)
    carried = lax.ppermute(jnp.sum(moment[:, None, :] * tail, axis=0), "handler",
                           [(i, i + 1) for i in range(n_handler - 1)])
    filtered = jnp.einsum("tj,ctp->cjp", lowpass[:, :local_j], by_component, preferred_element_type=jnp.float32)
    own = jnp.sum(moment[:, None, :] * filtered, axis=0)
    own = own.at[:halo].add(carried)
    by_time = lax.all_gather(own.astype(jnp.bfloat16), "handler", axis=0, tiled=True)
    length = by_time.shape[1]
    v_local, k = index.shape
    flat_index = jnp.clip(index.reshape(-1), 0, length - 1)
    choose = (flat_index[:, None] == lax.broadcasted_iota(jnp.int32, (flat_index.shape[0], length), 1))
    rows = jnp.einsum("np,jp->nj", choose.astype(jnp.bfloat16), by_time, preferred_element_type=jnp.float32)
    picked = rows.astype(jnp.bfloat16).reshape(v_local, k, by_time.shape[0])
    return convolve(picked, slip)


def solution(mesh):
    in_specs = (
        P(("site", "handler"), None, None),
        P(),
        P(),
        P("handler", None),
        P("handler", None, None),
    )
    out_specs = P(("site", "handler"), None)
    return jax.shard_map(body, mesh=mesh, in_specs=in_specs, out_specs=out_specs, check_vma=False)
```

```python
import jax
import jax.numpy as jnp
from jax import lax
from jax.experimental import pallas as pl
from jax.experimental.pallas import tpu as pltpu
from jax.sharding import PartitionSpec as P

DEC = 4
V_BLOCK = 16


def band_matrix(taps, rows, cols):
    n_taps = taps.shape[0]
    row_ids = lax.broadcasted_iota(jnp.int32, (rows, cols, n_taps), 0)
    col_ids = lax.broadcasted_iota(jnp.int32, (rows, cols, n_taps), 1)
    tap_ids = lax.broadcasted_iota(jnp.int32, (rows, cols, n_taps), 2)
    hit = DEC * col_ids - row_ids == tap_ids
    picked = jnp.where(hit, taps.astype(jnp.float32)[None, None, :], 0.0)
    return jnp.sum(picked, axis=2).astype(jnp.bfloat16)


SHIFTS = 4


def conv_kernel(weight_ref, picked_ref, out_ref, shifted_ref):
    vb = out_ref.shape[0]
    n_rows = weight_ref.shape[1]
    k = picked_ref.shape[1]
    width = out_ref.shape[1]
    edge = min(width, n_rows * SHIFTS)
    edge = -(-edge // 128) * 128
    col_in = lax.broadcasted_iota(jnp.int32, (k, 128), 1)
    col = lax.broadcasted_iota(jnp.int32, (8, edge), 1)
    row = lax.broadcasted_iota(jnp.int32, (8, edge), 0)
    lag = col - SHIFTS * row

    for v in range(vb):
        slot = v % 2
        rows = picked_ref[v]
        shifted_ref[slot, 0:k, :] = rows
        for b in range(1, SHIFTS):
            moved = pltpu.roll(rows, b, 1)
            shifted_ref[slot, b * k:(b + 1) * k, :128] = jnp.where(col_in >= b, moved[:, :128], jnp.zeros_like(moved[:, :128]))
            shifted_ref[slot, b * k:(b + 1) * k, 128:] = moved[:, 128:]
        spread = jnp.dot(weight_ref[v], shifted_ref[slot], preferred_element_type=jnp.float32)
        head = jnp.zeros((8, edge), jnp.float32)
        tail = jnp.zeros((8, width - edge), jnp.float32)
        for q in range(n_rows // 8):
            blk = spread[8 * q:8 * q + 8, :]
            moved = pltpu.roll(blk, 8 * SHIFTS * q, 1, stride=SHIFTS, stride_axis=0)
            head = head + jnp.where(lag >= 8 * SHIFTS * q, moved[:, :edge], 0.0)
            if width > edge:
                tail = tail + moved[:, edge:]
        out_ref[v:v + 1, :edge] = jnp.sum(head, axis=0, keepdims=True)
        if width > edge:
            out_ref[v:v + 1, edge:] = jnp.sum(tail, axis=0, keepdims=True)


def convolve(picked, slip):
    v_local, k, width = picked.shape
    span = slip.shape[2]
    n_rows = -(-span // SHIFTS)
    n_rows = -(-n_rows // 8) * 8
    padded = jnp.pad(slip, ((0, 0), (0, 0), (0, n_rows * SHIFTS - span)))
    weight = padded.reshape(v_local, k, n_rows, SHIFTS).transpose(0, 2, 3, 1).reshape(v_local, n_rows, SHIFTS * k)
    vb = min(V_BLOCK, v_local)
    return pl.pallas_call(
        conv_kernel,
        grid=(v_local // vb,),
        in_specs=[
            pl.BlockSpec((vb, n_rows, SHIFTS * k), lambda i: (i, 0, 0)),
            pl.BlockSpec((vb, k, width), lambda i: (i, 0, 0)),
        ],
        out_specs=pl.BlockSpec((vb, width), lambda i: (i, 0)),
        out_shape=jax.ShapeDtypeStruct((v_local, width), jnp.float32),
        scratch_shapes=[pltpu.VMEM((2, SHIFTS * k, width), jnp.bfloat16)],
    )(weight, picked)


def body(sgt, taps, moment, index, slip):
    n_handler = lax.axis_size("handler")
    me = lax.axis_index("handler")
    local_t = sgt.shape[0]
    local_j = local_t // DEC
    n_taps = taps.shape[0]
    halo = (n_taps - 1 + DEC - 1) // DEC
    lowpass = lax.optimization_barrier(band_matrix(taps, local_t, local_j + halo))
    by_component = jnp.transpose(sgt, (1, 0, 2))
    tail = jnp.einsum("tj,ctp->cjp", lowpass[local_t - n_taps:, local_j:], by_component[:, local_t - n_taps:, :],
                      preferred_element_type=jnp.float32)
    carried = lax.ppermute(jnp.sum(moment[:, None, :] * tail, axis=0), "handler",
                           [(i, i + 1) for i in range(n_handler - 1)])
    filtered = jnp.einsum("tj,ctp->cjp", lowpass[:, :local_j], by_component, preferred_element_type=jnp.float32)
    own = jnp.sum(moment[:, None, :] * filtered, axis=0)
    own = own.at[:halo].add(carried)
    by_time = lax.all_gather(own.astype(jnp.bfloat16), "handler", axis=0, tiled=True)
    length = by_time.shape[1]
    v_local, k = index.shape
    flat_index = jnp.clip(index.reshape(-1), 0, length - 1)
    choose = (flat_index[:, None] == lax.broadcasted_iota(jnp.int32, (flat_index.shape[0], length), 1))
    rows = jnp.einsum("np,jp->nj", choose.astype(jnp.bfloat16), by_time, preferred_element_type=jnp.float32)
    picked = rows.astype(jnp.bfloat16).reshape(v_local, k, by_time.shape[0])
    return convolve(picked, slip)


def solution(mesh):
    in_specs = (
        P(("site", "handler"), None, None),
        P(),
        P(),
        P("handler", None),
        P("handler", None, None),
    )
    out_specs = P(("site", "handler"), None)
    return jax.shard_map(body, mesh=mesh, in_specs=in_specs, out_specs=out_specs, check_vma=False)
```

```python
import jax
import jax.numpy as jnp
from jax import lax
from jax.experimental import pallas as pl
from jax.experimental.pallas import tpu as pltpu
from jax.sharding import PartitionSpec as P

DEC = 4
V_BLOCK = 8


def band_matrix(taps, rows, cols):
    n_taps = taps.shape[0]
    row_ids = lax.broadcasted_iota(jnp.int32, (rows, cols, n_taps), 0)
    col_ids = lax.broadcasted_iota(jnp.int32, (rows, cols, n_taps), 1)
    tap_ids = lax.broadcasted_iota(jnp.int32, (rows, cols, n_taps), 2)
    hit = DEC * col_ids - row_ids == tap_ids
    picked = jnp.where(hit, taps[None, None, :], jnp.zeros((), taps.dtype))
    return jnp.sum(picked, axis=2, dtype=jnp.bfloat16)


SHIFTS = 4


def conv_kernel(weight_ref, picked_ref, out_ref, shifted_ref):
    vb = out_ref.shape[0]
    n_rows = weight_ref.shape[1]
    k = picked_ref.shape[1]
    width = out_ref.shape[1]
    edge = min(width, n_rows * SHIFTS)
    edge = -(-edge // 128) * 128
    col_in = lax.broadcasted_iota(jnp.int32, (k, 128), 1)
    col = lax.broadcasted_iota(jnp.int32, (8, edge), 1)
    row = lax.broadcasted_iota(jnp.int32, (8, edge), 0)
    lag = col - SHIFTS * row

    for v in range(vb):
        slot = v % 2
        rows = picked_ref[v]
        shifted_ref[slot, 0:k, :] = rows
        for b in range(1, SHIFTS):
            moved = pltpu.roll(rows, b, 1)
            shifted_ref[slot, b * k:(b + 1) * k, :128] = jnp.where(col_in >= b, moved[:, :128], jnp.zeros_like(moved[:, :128]))
            shifted_ref[slot, b * k:(b + 1) * k, 128:] = moved[:, 128:]
        spread = jnp.dot(weight_ref[v], shifted_ref[slot], preferred_element_type=jnp.float32)
        head = jnp.zeros((8, edge), jnp.float32)
        tail = jnp.zeros((8, width - edge), jnp.float32)
        for q in range(n_rows // 8):
            blk = spread[8 * q:8 * q + 8, :]
            moved = pltpu.roll(blk, 8 * SHIFTS * q, 1, stride=SHIFTS, stride_axis=0)
            head = head + jnp.where(lag >= 8 * SHIFTS * q, moved[:, :edge], 0.0)
            if width > edge:
                tail = tail + moved[:, edge:]
        out_ref[v:v + 1, :edge] = jnp.sum(head, axis=0, keepdims=True)
        if width > edge:
            out_ref[v:v + 1, edge:] = jnp.sum(tail, axis=0, keepdims=True)


def convolve(picked, slip):
    v_local, k, width = picked.shape
    span = slip.shape[2]
    n_rows = -(-span // SHIFTS)
    n_rows = -(-n_rows // 8) * 8
    padded = jnp.pad(slip, ((0, 0), (0, 0), (0, n_rows * SHIFTS - span)))
    weight = padded.reshape(v_local, k, n_rows, SHIFTS).transpose(0, 2, 3, 1).reshape(v_local, n_rows, SHIFTS * k)
    vb = min(V_BLOCK, v_local)
    return pl.pallas_call(
        conv_kernel,
        grid=(v_local // vb,),
        in_specs=[
            pl.BlockSpec((vb, n_rows, SHIFTS * k), lambda i: (i, 0, 0)),
            pl.BlockSpec((vb, k, width), lambda i: (i, 0, 0)),
        ],
        out_specs=pl.BlockSpec((vb, width), lambda i: (i, 0)),
        out_shape=jax.ShapeDtypeStruct((v_local, width), jnp.float32),
        scratch_shapes=[pltpu.VMEM((2, SHIFTS * k, width), jnp.bfloat16)],
    )(weight, picked)


def body(sgt, taps, moment, index, slip):
    n_handler = lax.axis_size("handler")
    me = lax.axis_index("handler")
    local_t = sgt.shape[0]
    local_j = local_t // DEC
    n_taps = taps.shape[0]
    halo = (n_taps - 1 + DEC - 1) // DEC
    lowpass = lax.optimization_barrier(band_matrix(taps, local_t, local_j + halo))
    by_component = jnp.transpose(sgt, (1, 0, 2))
    tail = jnp.einsum("tj,ctp->cjp", lowpass[local_t - n_taps:, local_j:], by_component[:, local_t - n_taps:, :],
                      preferred_element_type=jnp.float32)
    carried = lax.ppermute(jnp.sum(moment[:, None, :] * tail, axis=0), "handler",
                           [(i, i + 1) for i in range(n_handler - 1)])
    filtered = jnp.einsum("tj,ctp->cjp", lowpass[:, :local_j], by_component, preferred_element_type=jnp.float32)
    own = jnp.sum(moment[:, None, :] * filtered, axis=0)
    green = (own + jnp.pad(carried, ((0, local_j - halo), (0, 0)))).astype(jnp.bfloat16)
    by_time = lax.all_gather(green, "handler", axis=0, tiled=True)
    length = by_time.shape[1]
    v_local, k = index.shape
    flat_index = jnp.clip(index.reshape(-1), 0, length - 1)
    choose = (flat_index[:, None] == lax.broadcasted_iota(jnp.int32, (flat_index.shape[0], length), 1))
    rows = jnp.einsum("np,jp->nj", choose.astype(jnp.bfloat16), by_time, preferred_element_type=jnp.float32)
    picked = rows.astype(jnp.bfloat16).reshape(v_local, k, by_time.shape[0])
    return convolve(picked, slip)


def solution(mesh):
    in_specs = (
        P(("site", "handler"), None, None),
        P(),
        P(),
        P("handler", None),
        P("handler", None, None),
    )
    out_specs = P(("site", "handler"), None)
    return jax.shard_map(body, mesh=mesh, in_specs=in_specs, out_specs=out_specs, check_vma=False)
```

```python
import jax
import jax.numpy as jnp
from jax import lax
from jax.experimental import pallas as pl
from jax.experimental.pallas import tpu as pltpu
from jax.sharding import PartitionSpec as P

DEC = 4
V_BLOCK = 8


def band_matrix(taps, rows, cols):
    n_taps = taps.shape[0]
    row_ids = lax.broadcasted_iota(jnp.int32, (rows, cols, n_taps), 0)
    col_ids = lax.broadcasted_iota(jnp.int32, (rows, cols, n_taps), 1)
    tap_ids = lax.broadcasted_iota(jnp.int32, (rows, cols, n_taps), 2)
    hit = DEC * col_ids - row_ids == tap_ids
    picked = jnp.where(hit, taps[None, None, :], jnp.zeros((), taps.dtype))
    return jnp.sum(picked, axis=2, dtype=jnp.bfloat16)


SHIFTS = 4


def conv_kernel(weight_ref, picked_ref, out_ref, shifted_ref):
    vb = out_ref.shape[0]
    n_rows = weight_ref.shape[1]
    k = picked_ref.shape[1]
    width = out_ref.shape[1]
    edge = min(width, n_rows * SHIFTS)
    edge = -(-edge // 128) * 128
    col_in = lax.broadcasted_iota(jnp.int32, (k, 128), 1)
    col = lax.broadcasted_iota(jnp.int32, (8, edge), 1)
    row = lax.broadcasted_iota(jnp.int32, (8, edge), 0)
    lag = col - SHIFTS * row

    for v in range(vb):
        slot = v % 2
        rows = picked_ref[v]
        shifted_ref[slot, 0:k, :] = rows
        for b in range(1, SHIFTS):
            moved = pltpu.roll(rows, b, 1)
            shifted_ref[slot, b * k:(b + 1) * k, :128] = jnp.where(col_in >= b, moved[:, :128], jnp.zeros_like(moved[:, :128]))
            shifted_ref[slot, b * k:(b + 1) * k, 128:] = moved[:, 128:]
        spread = jnp.dot(weight_ref[v], shifted_ref[slot], preferred_element_type=jnp.float32)
        head = jnp.zeros((8, edge), jnp.float32)
        tail = jnp.zeros((8, width - edge), jnp.float32)
        for q in range(n_rows // 8):
            blk = spread[8 * q:8 * q + 8, :]
            moved = pltpu.roll(blk, 8 * SHIFTS * q, 1, stride=SHIFTS, stride_axis=0)
            head = head + jnp.where(lag >= 8 * SHIFTS * q, moved[:, :edge], 0.0)
            if width > edge:
                tail = tail + moved[:, edge:]
        out_ref[v:v + 1, :edge] = jnp.sum(head, axis=0, keepdims=True)
        if width > edge:
            out_ref[v:v + 1, edge:] = jnp.sum(tail, axis=0, keepdims=True)


def convolve(picked, slip):
    v_local, k, width = picked.shape
    span = slip.shape[2]
    n_rows = -(-span // SHIFTS)
    n_rows = -(-n_rows // 8) * 8
    padded = jnp.pad(slip, ((0, 0), (0, 0), (0, n_rows * SHIFTS - span)))
    weight = padded.reshape(v_local, k, n_rows, SHIFTS).transpose(0, 2, 3, 1).reshape(v_local, n_rows, SHIFTS * k)
    vb = min(V_BLOCK, v_local)
    return pl.pallas_call(
        conv_kernel,
        grid=(v_local // vb,),
        in_specs=[
            pl.BlockSpec((vb, n_rows, SHIFTS * k), lambda i: (i, 0, 0)),
            pl.BlockSpec((vb, k, width), lambda i: (i, 0, 0)),
        ],
        out_specs=pl.BlockSpec((vb, width), lambda i: (i, 0)),
        out_shape=jax.ShapeDtypeStruct((v_local, width), jnp.float32),
        scratch_shapes=[pltpu.VMEM((2, SHIFTS * k, width), jnp.bfloat16)],
    )(weight, picked)


def body(sgt, taps, moment, index, slip):
    n_handler = lax.axis_size("handler")
    me = lax.axis_index("handler")
    local_t = sgt.shape[0]
    local_j = local_t // DEC
    n_taps = taps.shape[0]
    halo = (n_taps - 1 + DEC - 1) // DEC
    lowpass = lax.optimization_barrier(band_matrix(taps, local_t, local_j + halo))
    by_component = jnp.transpose(sgt, (1, 0, 2))
    filtered = jnp.einsum("tj,ctp->cjp", lowpass, by_component, preferred_element_type=jnp.float32)
    partial = jnp.sum(moment[:, None, :] * filtered, axis=0)
    carried = lax.ppermute(partial[local_j:], "handler", [(i, i + 1) for i in range(n_handler - 1)])
    own = partial[:local_j]
    green = (own + jnp.pad(carried, ((0, local_j - halo), (0, 0)))).astype(jnp.bfloat16)
    by_time = lax.all_gather(green, "handler", axis=0, tiled=True)
    length = by_time.shape[1]
    v_local, k = index.shape
    flat_index = jnp.clip(index.reshape(-1), 0, length - 1)
    choose = (flat_index[:, None] == lax.broadcasted_iota(jnp.int32, (flat_index.shape[0], length), 1))
    rows = jnp.einsum("np,jp->nj", choose.astype(jnp.bfloat16), by_time, preferred_element_type=jnp.float32)
    picked = rows.astype(jnp.bfloat16).reshape(v_local, k, by_time.shape[0])
    return convolve(picked, slip)


def solution(mesh):
    in_specs = (
        P(("site", "handler"), None, None),
        P(),
        P(),
        P("handler", None),
        P("handler", None, None),
    )
    out_specs = P(("site", "handler"), None)
    return jax.shard_map(body, mesh=mesh, in_specs=in_specs, out_specs=out_specs, check_vma=False)
```

```python
import jax
import jax.numpy as jnp
from jax import lax
from jax.experimental import pallas as pl
from jax.experimental.pallas import tpu as pltpu
from jax.sharding import PartitionSpec as P

DEC = 4
V_BLOCK = 8


def band_matrix(taps, rows, cols):
    n_taps = taps.shape[0]
    row_ids = lax.broadcasted_iota(jnp.int32, (rows, cols, n_taps), 0)
    col_ids = lax.broadcasted_iota(jnp.int32, (rows, cols, n_taps), 1)
    tap_ids = lax.broadcasted_iota(jnp.int32, (rows, cols, n_taps), 2)
    hit = DEC * col_ids - row_ids == tap_ids
    picked = jnp.where(hit, taps.astype(jnp.float32)[None, None, :], 0.0)
    return jnp.sum(picked, axis=2).astype(jnp.bfloat16)


SHIFTS = 4


def conv_kernel(weight_ref, picked_ref, out_ref, shifted_ref, acc_ref):
    vb = out_ref.shape[0]
    n_rows = weight_ref.shape[1]
    k = picked_ref.shape[1]
    width = out_ref.shape[1]
    edge = min(width, n_rows * SHIFTS)
    edge = -(-edge // 128) * 128
    col_in = lax.broadcasted_iota(jnp.int32, (k, 128), 1)
    col = lax.broadcasted_iota(jnp.int32, (8, edge), 1)
    row = lax.broadcasted_iota(jnp.int32, (8, edge), 0)
    lag = col - SHIFTS * row

    for v in range(vb):
        slot = v % 2
        rows = picked_ref[v]
        shifted_ref[slot, 0:k, :] = rows
        for b in range(1, SHIFTS):
            moved = pltpu.roll(rows, b, 1)
            shifted_ref[slot, b * k:(b + 1) * k, :128] = jnp.where(col_in >= b, moved[:, :128], jnp.zeros_like(moved[:, :128]))
            shifted_ref[slot, b * k:(b + 1) * k, 128:] = moved[:, 128:]
        spread = jnp.dot(weight_ref[v], shifted_ref[slot], preferred_element_type=jnp.float32)
        head = jnp.zeros((8, edge), jnp.float32)
        tail = jnp.zeros((8, width - edge), jnp.float32)
        for q in range(n_rows // 8):
            blk = spread[8 * q:8 * q + 8, :]
            moved = pltpu.roll(blk, 8 * SHIFTS * q, 1, stride=SHIFTS, stride_axis=0)
            head = head + jnp.where(lag >= 8 * SHIFTS * q, moved[:, :edge], 0.0)
            if width > edge:
                tail = tail + moved[:, edge:]
        for t in range(edge // 128):
            acc_ref[t, 8 * v:8 * v + 8, :] = head[:, 128 * t:128 * (t + 1)]
        for t in range((width - edge) // 128):
            acc_ref[edge // 128 + t, 8 * v:8 * v + 8, :] = tail[:, 128 * t:128 * (t + 1)]
    for t in range(width // 128):
        total = acc_ref[t, pl.ds(0, vb, stride=8), :]
        for s in range(1, 8):
            total = total + acc_ref[t, pl.ds(s, vb, stride=8), :]
        out_ref[:, 128 * t:128 * (t + 1)] = total


def convolve(picked, slip):
    v_local, k, width = picked.shape
    span = slip.shape[2]
    n_rows = -(-span // SHIFTS)
    n_rows = -(-n_rows // 8) * 8
    padded = jnp.pad(slip, ((0, 0), (0, 0), (0, n_rows * SHIFTS - span)))
    weight = padded.reshape(v_local, k, n_rows, SHIFTS).transpose(0, 2, 3, 1).reshape(v_local, n_rows, SHIFTS * k)
    vb = min(V_BLOCK, v_local)
    return pl.pallas_call(
        conv_kernel,
        grid=(v_local // vb,),
        in_specs=[
            pl.BlockSpec((vb, n_rows, SHIFTS * k), lambda i: (i, 0, 0)),
            pl.BlockSpec((vb, k, width), lambda i: (i, 0, 0)),
        ],
        out_specs=pl.BlockSpec((vb, width), lambda i: (i, 0)),
        out_shape=jax.ShapeDtypeStruct((v_local, width), jnp.float32),
        scratch_shapes=[pltpu.VMEM((2, SHIFTS * k, width), jnp.bfloat16), pltpu.VMEM((width // 128, 8 * vb, 128), jnp.float32)],
    )(weight, picked)


def body(sgt, taps, moment, index, slip):
    n_handler = lax.axis_size("handler")
    me = lax.axis_index("handler")
    local_t = sgt.shape[0]
    local_j = local_t // DEC
    n_taps = taps.shape[0]
    halo = (n_taps - 1 + DEC - 1) // DEC
    lowpass = lax.optimization_barrier(band_matrix(taps, local_t, local_j + halo))
    by_component = jnp.transpose(sgt, (1, 0, 2))
    tail = jnp.einsum("tj,ctp->cjp", lowpass[local_t - n_taps:, local_j:], by_component[:, local_t - n_taps:, :],
                      preferred_element_type=jnp.float32)
    carried = lax.ppermute(jnp.sum(moment[:, None, :] * tail, axis=0), "handler",
                           [(i, i + 1) for i in range(n_handler - 1)])
    filtered = jnp.einsum("tj,ctp->cjp", lowpass[:, :local_j], by_component, preferred_element_type=jnp.float32)
    own = jnp.sum(moment[:, None, :] * filtered, axis=0)
    own = own.at[:halo].add(carried)
    by_time = lax.all_gather(own.astype(jnp.bfloat16), "handler", axis=0, tiled=True)
    length = by_time.shape[1]
    v_local, k = index.shape
    flat_index = jnp.clip(index.reshape(-1), 0, length - 1)
    choose = (flat_index[:, None] == lax.broadcasted_iota(jnp.int32, (flat_index.shape[0], length), 1))
    rows = jnp.einsum("np,jp->nj", choose.astype(jnp.bfloat16), by_time, preferred_element_type=jnp.float32)
    picked = rows.astype(jnp.bfloat16).reshape(v_local, k, by_time.shape[0])
    return convolve(picked, slip)


def solution(mesh):
    in_specs = (
        P(("site", "handler"), None, None),
        P(),
        P(),
        P("handler", None),
        P("handler", None, None),
    )
    out_specs = P(("site", "handler"), None)
    return jax.shard_map(body, mesh=mesh, in_specs=in_specs, out_specs=out_specs, check_vma=False)
```

```python
import jax
import jax.numpy as jnp
from jax import lax
from jax.experimental import pallas as pl
from jax.experimental.pallas import tpu as pltpu
from jax.sharding import PartitionSpec as P

DEC = 4
V_BLOCK = 16


def band_matrix(taps, rows, cols):
    n_taps = taps.shape[0]
    row_ids = lax.broadcasted_iota(jnp.int32, (rows, cols, n_taps), 0)
    col_ids = lax.broadcasted_iota(jnp.int32, (rows, cols, n_taps), 1)
    tap_ids = lax.broadcasted_iota(jnp.int32, (rows, cols, n_taps), 2)
    hit = DEC * col_ids - row_ids == tap_ids
    picked = jnp.where(hit, taps.astype(jnp.float32)[None, None, :], 0.0)
    return jnp.sum(picked, axis=2).astype(jnp.bfloat16)


SHIFTS = 4


def conv_kernel(weight_ref, picked_ref, out_ref, shifted_ref, acc_ref):
    vb = out_ref.shape[0]
    n_rows = weight_ref.shape[1]
    k = picked_ref.shape[1]
    width = out_ref.shape[1]
    edge = min(width, n_rows * SHIFTS)
    edge = -(-edge // 128) * 128
    col_in = lax.broadcasted_iota(jnp.int32, (k, 128), 1)
    col = lax.broadcasted_iota(jnp.int32, (8, edge), 1)
    row = lax.broadcasted_iota(jnp.int32, (8, edge), 0)
    lag = col - SHIFTS * row

    for v in range(vb):
        slot = v % 2
        rows = picked_ref[v]
        shifted_ref[slot, 0:k, :] = rows
        for b in range(1, SHIFTS):
            moved = pltpu.roll(rows, b, 1)
            shifted_ref[slot, b * k:(b + 1) * k, :128] = jnp.where(col_in >= b, moved[:, :128], jnp.zeros_like(moved[:, :128]))
            shifted_ref[slot, b * k:(b + 1) * k, 128:] = moved[:, 128:]
        spread = jnp.dot(weight_ref[v], shifted_ref[slot], preferred_element_type=jnp.float32)
        head = jnp.zeros((8, edge), jnp.float32)
        tail = jnp.zeros((8, width - edge), jnp.float32)
        for q in range(n_rows // 8):
            blk = spread[8 * q:8 * q + 8, :]
            moved = pltpu.roll(blk, 8 * SHIFTS * q, 1, stride=SHIFTS, stride_axis=0)
            head = head + jnp.where(lag >= 8 * SHIFTS * q, moved[:, :edge], 0.0)
            if width > edge:
                tail = tail + moved[:, edge:]
        for t in range(edge // 128):
            acc_ref[t, 8 * v:8 * v + 8, :] = head[:, 128 * t:128 * (t + 1)]
        for t in range((width - edge) // 128):
            acc_ref[edge // 128 + t, 8 * v:8 * v + 8, :] = tail[:, 128 * t:128 * (t + 1)]
    for t in range(width // 128):
        total = acc_ref[t, pl.ds(0, vb, stride=8), :]
        for s in range(1, 8):
            total = total + acc_ref[t, pl.ds(s, vb, stride=8), :]
        out_ref[:, 128 * t:128 * (t + 1)] = total


def convolve(picked, slip):
    v_local, k, width = picked.shape
    span = slip.shape[2]
    n_rows = -(-span // SHIFTS)
    n_rows = -(-n_rows // 8) * 8
    padded = jnp.pad(slip, ((0, 0), (0, 0), (0, n_rows * SHIFTS - span)))
    weight = padded.reshape(v_local, k, n_rows, SHIFTS).transpose(0, 2, 3, 1).reshape(v_local, n_rows, SHIFTS * k)
    vb = min(V_BLOCK, v_local)
    return pl.pallas_call(
        conv_kernel,
        grid=(v_local // vb,),
        in_specs=[
            pl.BlockSpec((vb, n_rows, SHIFTS * k), lambda i: (i, 0, 0)),
            pl.BlockSpec((vb, k, width), lambda i: (i, 0, 0)),
        ],
        out_specs=pl.BlockSpec((vb, width), lambda i: (i, 0)),
        out_shape=jax.ShapeDtypeStruct((v_local, width), jnp.float32),
        scratch_shapes=[pltpu.VMEM((2, SHIFTS * k, width), jnp.bfloat16), pltpu.VMEM((width // 128, 8 * vb, 128), jnp.float32)],
    )(weight, picked)


def body(sgt, taps, moment, index, slip):
    n_handler = lax.axis_size("handler")
    me = lax.axis_index("handler")
    local_t = sgt.shape[0]
    local_j = local_t // DEC
    n_taps = taps.shape[0]
    halo = (n_taps - 1 + DEC - 1) // DEC
    lowpass = lax.optimization_barrier(band_matrix(taps, local_t, local_j + halo))
    by_component = jnp.transpose(sgt, (1, 0, 2))
    tail = jnp.einsum("tj,ctp->cjp", lowpass[local_t - n_taps:, local_j:], by_component[:, local_t - n_taps:, :],
                      preferred_element_type=jnp.float32)
    carried = lax.ppermute(jnp.sum(moment[:, None, :] * tail, axis=0), "handler",
                           [(i, i + 1) for i in range(n_handler - 1)])
    filtered = jnp.einsum("tj,ctp->cjp", lowpass[:, :local_j], by_component, preferred_element_type=jnp.float32)
    own = jnp.sum(moment[:, None, :] * filtered, axis=0)
    own = own.at[:halo].add(carried)
    by_time = lax.all_gather(own.astype(jnp.bfloat16), "handler", axis=0, tiled=True)
    length = by_time.shape[1]
    v_local, k = index.shape
    flat_index = jnp.clip(index.reshape(-1), 0, length - 1)
    choose = (flat_index[:, None] == lax.broadcasted_iota(jnp.int32, (flat_index.shape[0], length), 1))
    rows = jnp.einsum("np,jp->nj", choose.astype(jnp.bfloat16), by_time, preferred_element_type=jnp.float32)
    picked = rows.astype(jnp.bfloat16).reshape(v_local, k, by_time.shape[0])
    return convolve(picked, slip)


def solution(mesh):
    in_specs = (
        P(("site", "handler"), None, None),
        P(),
        P(),
        P("handler", None),
        P("handler", None, None),
    )
    out_specs = P(("site", "handler"), None)
    return jax.shard_map(body, mesh=mesh, in_specs=in_specs, out_specs=out_specs, check_vma=False)
```

```python
import jax
import jax.numpy as jnp
from jax import lax
from jax.experimental import pallas as pl
from jax.experimental.pallas import tpu as pltpu
from jax.sharding import PartitionSpec as P

DEC = 4
V_BLOCK = 8


def band_matrix(taps, rows, cols):
    n_taps = taps.shape[0]
    row_ids = lax.broadcasted_iota(jnp.int32, (rows, cols, n_taps), 0)
    col_ids = lax.broadcasted_iota(jnp.int32, (rows, cols, n_taps), 1)
    tap_ids = lax.broadcasted_iota(jnp.int32, (rows, cols, n_taps), 2)
    hit = DEC * col_ids - row_ids == tap_ids
    picked = jnp.where(hit, taps[None, None, :], jnp.zeros((), taps.dtype)).astype(jnp.float32)
    return jnp.sum(picked, axis=2).astype(jnp.bfloat16)


SHIFTS = 4


def conv_kernel(weight_ref, picked_ref, out_ref, shifted_ref, acc_ref):
    vb = out_ref.shape[0]
    n_rows = weight_ref.shape[1]
    k = picked_ref.shape[1]
    width = out_ref.shape[1]
    edge = min(width, n_rows * SHIFTS)
    edge = -(-edge // 128) * 128
    col_in = lax.broadcasted_iota(jnp.int32, (k, 128), 1)
    col = lax.broadcasted_iota(jnp.int32, (8, edge), 1)
    row = lax.broadcasted_iota(jnp.int32, (8, edge), 0)
    lag = col - SHIFTS * row

    for v in range(vb):
        slot = v % 2
        rows = picked_ref[v]
        shifted_ref[slot, 0:k, :] = rows
        for b in range(1, SHIFTS):
            moved = pltpu.roll(rows, b, 1)
            shifted_ref[slot, b * k:(b + 1) * k, :128] = jnp.where(col_in >= b, moved[:, :128], jnp.zeros_like(moved[:, :128]))
            shifted_ref[slot, b * k:(b + 1) * k, 128:] = moved[:, 128:]
        spread = jnp.dot(weight_ref[v], shifted_ref[slot], preferred_element_type=jnp.float32)
        head = jnp.zeros((8, edge), jnp.float32)
        tail = jnp.zeros((8, width - edge), jnp.float32)
        for q in range(n_rows // 8):
            blk = spread[8 * q:8 * q + 8, :]
            moved = pltpu.roll(blk, 8 * SHIFTS * q, 1, stride=SHIFTS, stride_axis=0)
            head = head + jnp.where(lag >= 8 * SHIFTS * q, moved[:, :edge], 0.0)
            if width > edge:
                tail = tail + moved[:, edge:]
        for t in range(edge // 128):
            acc_ref[t, 8 * v:8 * v + 8, :] = head[:, 128 * t:128 * (t + 1)]
        for t in range((width - edge) // 128):
            acc_ref[edge // 128 + t, 8 * v:8 * v + 8, :] = tail[:, 128 * t:128 * (t + 1)]
    for t in range(width // 128):
        total = acc_ref[t, pl.ds(0, vb, stride=8), :]
        for s in range(1, 8):
            total = total + acc_ref[t, pl.ds(s, vb, stride=8), :]
        out_ref[:, 128 * t:128 * (t + 1)] = total


def convolve(picked, slip):
    v_local, k, width = picked.shape
    span = slip.shape[2]
    n_rows = -(-span // SHIFTS)
    n_rows = -(-n_rows // 8) * 8
    padded = jnp.pad(slip, ((0, 0), (0, 0), (0, n_rows * SHIFTS - span)))
    weight = padded.reshape(v_local, k, n_rows, SHIFTS).transpose(0, 2, 3, 1).reshape(v_local, n_rows, SHIFTS * k)
    vb = min(V_BLOCK, v_local)
    return pl.pallas_call(
        conv_kernel,
        grid=(v_local // vb,),
        in_specs=[
            pl.BlockSpec((vb, n_rows, SHIFTS * k), lambda i: (i, 0, 0)),
            pl.BlockSpec((vb, k, width), lambda i: (i, 0, 0)),
        ],
        out_specs=pl.BlockSpec((vb, width), lambda i: (i, 0)),
        out_shape=jax.ShapeDtypeStruct((v_local, width), jnp.float32),
        scratch_shapes=[pltpu.VMEM((2, SHIFTS * k, width), jnp.bfloat16), pltpu.VMEM((width // 128, 8 * vb, 128), jnp.float32)],
    )(weight, picked)


def body(sgt, taps, moment, index, slip):
    n_handler = lax.axis_size("handler")
    me = lax.axis_index("handler")
    local_t = sgt.shape[0]
    local_j = local_t // DEC
    n_taps = taps.shape[0]
    halo = (n_taps - 1 + DEC - 1) // DEC
    lowpass = lax.optimization_barrier(band_matrix(taps, local_t, local_j + halo))
    by_component = jnp.transpose(sgt, (1, 0, 2))
    tail = jnp.einsum("tj,ctp->cjp", lowpass[local_t - n_taps:, local_j:], by_component[:, local_t - n_taps:, :],
                      preferred_element_type=jnp.float32)
    carried = lax.ppermute(jnp.sum(moment[:, None, :] * tail, axis=0), "handler",
                           [(i, i + 1) for i in range(n_handler - 1)])
    filtered = jnp.einsum("tj,ctp->cjp", lowpass[:, :local_j], by_component, preferred_element_type=jnp.float32)
    own = jnp.sum(moment[:, None, :] * filtered, axis=0)
    own = own.at[:halo].add(carried)
    by_time = lax.all_gather(own.astype(jnp.bfloat16), "handler", axis=0, tiled=True)
    length = by_time.shape[1]
    v_local, k = index.shape
    flat_index = jnp.clip(index.reshape(-1), 0, length - 1)
    choose = (flat_index[:, None] == lax.broadcasted_iota(jnp.int32, (flat_index.shape[0], length), 1))
    rows = jnp.einsum("np,jp->nj", choose.astype(jnp.bfloat16), by_time, preferred_element_type=jnp.float32)
    picked = rows.astype(jnp.bfloat16).reshape(v_local, k, by_time.shape[0])
    return convolve(picked, slip)


def solution(mesh):
    in_specs = (
        P(("site", "handler"), None, None),
        P(),
        P(),
        P("handler", None),
        P("handler", None, None),
    )
    out_specs = P(("site", "handler"), None)
    return jax.shard_map(body, mesh=mesh, in_specs=in_specs, out_specs=out_specs, check_vma=False)
```

```python
import jax
import jax.numpy as jnp
from jax import lax
from jax.experimental import pallas as pl
from jax.experimental.pallas import tpu as pltpu
from jax.sharding import PartitionSpec as P

DEC = 4
V_BLOCK = 8


def band_matrix(taps, rows, cols):
    n_taps = taps.shape[0]
    span = -(-(n_taps + DEC - 1) // DEC)
    padded = jnp.pad(taps, (DEC - 1, span * DEC - n_taps - DEC + 1))
    phase = padded.reshape(span, DEC)[:, ::-1].T
    s_ids = lax.broadcasted_iota(jnp.int32, (rows // DEC, DEC, cols), 0)
    j_ids = lax.broadcasted_iota(jnp.int32, (rows // DEC, DEC, cols), 2)
    lag = j_ids - s_ids
    matrix = jnp.zeros((rows // DEC, DEC, cols), taps.dtype)
    for d in range(span):
        matrix = jnp.where(lag == d, phase[None, :, d, None], matrix)
    return matrix.reshape(rows, cols)


SHIFTS = 4


def conv_kernel(weight_ref, picked_ref, out_ref, shifted_ref, acc_ref):
    vb = out_ref.shape[0]
    n_rows = weight_ref.shape[1]
    k = picked_ref.shape[1]
    width = out_ref.shape[1]
    edge = min(width, n_rows * SHIFTS)
    edge = -(-edge // 128) * 128
    col_in = lax.broadcasted_iota(jnp.int32, (k, 128), 1)
    col = lax.broadcasted_iota(jnp.int32, (8, edge), 1)
    row = lax.broadcasted_iota(jnp.int32, (8, edge), 0)
    lag = col - SHIFTS * row

    for v in range(vb):
        slot = v % 2
        rows = picked_ref[v]
        shifted_ref[slot, 0:k, :] = rows
        for b in range(1, SHIFTS):
            moved = pltpu.roll(rows, b, 1)
            shifted_ref[slot, b * k:(b + 1) * k, :128] = jnp.where(col_in >= b, moved[:, :128], jnp.zeros_like(moved[:, :128]))
            shifted_ref[slot, b * k:(b + 1) * k, 128:] = moved[:, 128:]
        spread = jnp.dot(weight_ref[v], shifted_ref[slot], preferred_element_type=jnp.float32)
        head = jnp.zeros((8, edge), jnp.float32)
        tail = jnp.zeros((8, width - edge), jnp.float32)
        for q in range(n_rows // 8):
            blk = spread[8 * q:8 * q + 8, :]
            moved = pltpu.roll(blk, 8 * SHIFTS * q, 1, stride=SHIFTS, stride_axis=0)
            head = head + jnp.where(lag >= 8 * SHIFTS * q, moved[:, :edge], 0.0)
            if width > edge:
                tail = tail + moved[:, edge:]
        for t in range(edge // 128):
            acc_ref[t, 8 * v:8 * v + 8, :] = head[:, 128 * t:128 * (t + 1)]
        for t in range((width - edge) // 128):
            acc_ref[edge // 128 + t, 8 * v:8 * v + 8, :] = tail[:, 128 * t:128 * (t + 1)]
    for t in range(width // 128):
        total = acc_ref[t, pl.ds(0, vb, stride=8), :]
        for s in range(1, 8):
            total = total + acc_ref[t, pl.ds(s, vb, stride=8), :]
        out_ref[:, 128 * t:128 * (t + 1)] = total


def convolve(picked, slip):
    v_local, k, width = picked.shape
    span = slip.shape[2]
    n_rows = -(-span // SHIFTS)
    n_rows = -(-n_rows // 8) * 8
    padded = jnp.pad(slip, ((0, 0), (0, 0), (0, n_rows * SHIFTS - span)))
    weight = padded.reshape(v_local, k, n_rows, SHIFTS).transpose(0, 2, 3, 1).reshape(v_local, n_rows, SHIFTS * k)
    vb = min(V_BLOCK, v_local)
    return pl.pallas_call(
        conv_kernel,
        grid=(v_local // vb,),
        in_specs=[
            pl.BlockSpec((vb, n_rows, SHIFTS * k), lambda i: (i, 0, 0)),
            pl.BlockSpec((vb, k, width), lambda i: (i, 0, 0)),
        ],
        out_specs=pl.BlockSpec((vb, width), lambda i: (i, 0)),
        out_shape=jax.ShapeDtypeStruct((v_local, width), jnp.float32),
        scratch_shapes=[pltpu.VMEM((2, SHIFTS * k, width), jnp.bfloat16), pltpu.VMEM((width // 128, 8 * vb, 128), jnp.float32)],
    )(weight, picked)


def body(sgt, taps, moment, index, slip):
    n_handler = lax.axis_size("handler")
    me = lax.axis_index("handler")
    local_t = sgt.shape[0]
    local_j = local_t // DEC
    n_taps = taps.shape[0]
    halo = (n_taps - 1 + DEC - 1) // DEC
    lowpass = lax.optimization_barrier(band_matrix(taps, local_t, local_j + halo))
    by_component = jnp.transpose(sgt, (1, 0, 2))
    tail = jnp.einsum("tj,ctp->cjp", lowpass[local_t - n_taps:, local_j:], by_component[:, local_t - n_taps:, :],
                      preferred_element_type=jnp.float32)
    carried = lax.ppermute(jnp.sum(moment[:, None, :] * tail, axis=0), "handler",
                           [(i, i + 1) for i in range(n_handler - 1)])
    filtered = jnp.einsum("tj,ctp->cjp", lowpass[:, :local_j], by_component, preferred_element_type=jnp.float32)
    own = jnp.sum(moment[:, None, :] * filtered, axis=0)
    own = own.at[:halo].add(carried)
    by_time = lax.all_gather(own.astype(jnp.bfloat16), "handler", axis=0, tiled=True)
    length = by_time.shape[1]
    v_local, k = index.shape
    flat_index = jnp.clip(index.reshape(-1), 0, length - 1)
    choose = (flat_index[:, None] == lax.broadcasted_iota(jnp.int32, (flat_index.shape[0], length), 1))
    rows = jnp.einsum("np,jp->nj", choose.astype(jnp.bfloat16), by_time, preferred_element_type=jnp.float32)
    picked = rows.astype(jnp.bfloat16).reshape(v_local, k, by_time.shape[0])
    return convolve(picked, slip)


def solution(mesh):
    in_specs = (
        P(("site", "handler"), None, None),
        P(),
        P(),
        P("handler", None),
        P("handler", None, None),
    )
    out_specs = P(("site", "handler"), None)
    return jax.shard_map(body, mesh=mesh, in_specs=in_specs, out_specs=out_specs, check_vma=False)
```

```python
import jax
import jax.numpy as jnp
from jax import lax
from jax.experimental import pallas as pl
from jax.experimental.pallas import tpu as pltpu
from jax.sharding import PartitionSpec as P

DEC = 4
V_BLOCK = 8


def band_matrix(taps, rows, cols):
    n_taps = taps.shape[0]
    span = -(-(n_taps + DEC - 1) // DEC)
    s_ids = lax.broadcasted_iota(jnp.int32, (rows // DEC, DEC, cols), 0)
    j_ids = lax.broadcasted_iota(jnp.int32, (rows // DEC, DEC, cols), 2)
    lag = j_ids - s_ids
    matrix = jnp.zeros((rows // DEC, DEC, cols), taps.dtype)
    for d in range(span):
        low, high = DEC * d - DEC + 1, DEC * d + 1
        column = taps[max(low, 0):min(high, n_taps)][::-1]
        column = jnp.concatenate([jnp.zeros((max(high - n_taps, 0),), taps.dtype), column,
                                  jnp.zeros((max(-low, 0),), taps.dtype)])
        matrix = jnp.where(lag == d, column[None, :, None], matrix)
    return matrix.reshape(rows, cols)


SHIFTS = 4


def conv_kernel(weight_ref, picked_ref, out_ref, shifted_ref, acc_ref):
    vb = out_ref.shape[0]
    n_rows = weight_ref.shape[1]
    k = picked_ref.shape[1]
    width = out_ref.shape[1]
    edge = min(width, n_rows * SHIFTS)
    edge = -(-edge // 128) * 128
    col_in = lax.broadcasted_iota(jnp.int32, (k, 128), 1)
    col = lax.broadcasted_iota(jnp.int32, (8, edge), 1)
    row = lax.broadcasted_iota(jnp.int32, (8, edge), 0)
    lag = col - SHIFTS * row

    for v in range(vb):
        slot = v % 2
        rows = picked_ref[v]
        shifted_ref[slot, 0:k, :] = rows
        for b in range(1, SHIFTS):
            moved = pltpu.roll(rows, b, 1)
            shifted_ref[slot, b * k:(b + 1) * k, :128] = jnp.where(col_in >= b, moved[:, :128], jnp.zeros_like(moved[:, :128]))
            shifted_ref[slot, b * k:(b + 1) * k, 128:] = moved[:, 128:]
        spread = jnp.dot(weight_ref[v], shifted_ref[slot], preferred_element_type=jnp.float32)
        head = jnp.zeros((8, edge), jnp.float32)
        tail = jnp.zeros((8, width - edge), jnp.float32)
        for q in range(n_rows // 8):
            blk = spread[8 * q:8 * q + 8, :]
            moved = pltpu.roll(blk, 8 * SHIFTS * q, 1, stride=SHIFTS, stride_axis=0)
            head = head + jnp.where(lag >= 8 * SHIFTS * q, moved[:, :edge], 0.0)
            if width > edge:
                tail = tail + moved[:, edge:]
        for t in range(edge // 128):
            acc_ref[t, 8 * v:8 * v + 8, :] = head[:, 128 * t:128 * (t + 1)]
        for t in range((width - edge) // 128):
            acc_ref[edge // 128 + t, 8 * v:8 * v + 8, :] = tail[:, 128 * t:128 * (t + 1)]
    for t in range(width // 128):
        total = acc_ref[t, pl.ds(0, vb, stride=8), :]
        for s in range(1, 8):
            total = total + acc_ref[t, pl.ds(s, vb, stride=8), :]
        out_ref[:, 128 * t:128 * (t + 1)] = total


def convolve(picked, slip):
    v_local, k, width = picked.shape
    span = slip.shape[2]
    n_rows = -(-span // SHIFTS)
    n_rows = -(-n_rows // 8) * 8
    padded = jnp.pad(slip, ((0, 0), (0, 0), (0, n_rows * SHIFTS - span)))
    weight = padded.reshape(v_local, k, n_rows, SHIFTS).transpose(0, 2, 3, 1).reshape(v_local, n_rows, SHIFTS * k)
    vb = min(V_BLOCK, v_local)
    return pl.pallas_call(
        conv_kernel,
        grid=(v_local // vb,),
        in_specs=[
            pl.BlockSpec((vb, n_rows, SHIFTS * k), lambda i: (i, 0, 0)),
            pl.BlockSpec((vb, k, width), lambda i: (i, 0, 0)),
        ],
        out_specs=pl.BlockSpec((vb, width), lambda i: (i, 0)),
        out_shape=jax.ShapeDtypeStruct((v_local, width), jnp.float32),
        scratch_shapes=[pltpu.VMEM((2, SHIFTS * k, width), jnp.bfloat16), pltpu.VMEM((width // 128, 8 * vb, 128), jnp.float32)],
    )(weight, picked)


def body(sgt, taps, moment, index, slip):
    n_handler = lax.axis_size("handler")
    me = lax.axis_index("handler")
    local_t = sgt.shape[0]
    local_j = local_t // DEC
    n_taps = taps.shape[0]
    halo = (n_taps - 1 + DEC - 1) // DEC
    lowpass = lax.optimization_barrier(band_matrix(taps, local_t, local_j + halo))
    by_component = jnp.transpose(sgt, (1, 0, 2))
    tail = jnp.einsum("tj,ctp->cjp", lowpass[local_t - n_taps:, local_j:], by_component[:, local_t - n_taps:, :],
                      preferred_element_type=jnp.float32)
    carried = lax.ppermute(jnp.sum(moment[:, None, :] * tail, axis=0), "handler",
                           [(i, i + 1) for i in range(n_handler - 1)])
    filtered = jnp.einsum("tj,ctp->cjp", lowpass[:, :local_j], by_component, preferred_element_type=jnp.float32)
    own = jnp.sum(moment[:, None, :] * filtered, axis=0)
    own = own.at[:halo].add(carried)
    by_time = lax.all_gather(own.astype(jnp.bfloat16), "handler", axis=0, tiled=True)
    length = by_time.shape[1]
    v_local, k = index.shape
    flat_index = jnp.clip(index.reshape(-1), 0, length - 1)
    choose = (flat_index[:, None] == lax.broadcasted_iota(jnp.int32, (flat_index.shape[0], length), 1))
    rows = jnp.einsum("np,jp->nj", choose.astype(jnp.bfloat16), by_time, preferred_element_type=jnp.float32)
    picked = rows.astype(jnp.bfloat16).reshape(v_local, k, by_time.shape[0])
    return convolve(picked, slip)


def solution(mesh):
    in_specs = (
        P(("site", "handler"), None, None),
        P(),
        P(),
        P("handler", None),
        P("handler", None, None),
    )
    out_specs = P(("site", "handler"), None)
    return jax.shard_map(body, mesh=mesh, in_specs=in_specs, out_specs=out_specs, check_vma=False)
```

```python
import jax
import jax.numpy as jnp
from jax import lax
from jax.experimental import pallas as pl
from jax.experimental.pallas import tpu as pltpu
from jax.sharding import PartitionSpec as P

DEC = 4
V_BLOCK = 8


def band_matrix(taps, rows, cols):
    n_taps = taps.shape[0]
    row_ids = lax.broadcasted_iota(jnp.int32, (rows, cols, n_taps), 0)
    col_ids = lax.broadcasted_iota(jnp.int32, (rows, cols, n_taps), 1)
    tap_ids = lax.broadcasted_iota(jnp.int32, (rows, cols, n_taps), 2)
    hit = DEC * col_ids - row_ids == tap_ids
    picked = jnp.where(hit, taps.astype(jnp.float32)[None, None, :], 0.0)
    return jnp.sum(picked, axis=2).astype(jnp.bfloat16)


SHIFTS = 4


def conv_kernel(weight_ref, picked_ref, out_ref, shifted_ref, acc_ref):
    vb = out_ref.shape[0]
    n_rows = weight_ref.shape[1]
    k = picked_ref.shape[1]
    width = out_ref.shape[1]
    edge = min(width, n_rows * SHIFTS)
    edge = -(-edge // 128) * 128
    col_in = lax.broadcasted_iota(jnp.int32, (k, 128), 1)
    col = lax.broadcasted_iota(jnp.int32, (8, edge), 1)
    row = lax.broadcasted_iota(jnp.int32, (8, edge), 0)
    lag = col - SHIFTS * row

    for v in range(vb):
        slot = v % 3
        rows = picked_ref[v]
        shifted_ref[slot, 0:k, :] = rows
        for b in range(1, SHIFTS):
            moved = pltpu.roll(rows, b, 1)
            shifted_ref[slot, b * k:(b + 1) * k, :128] = jnp.where(col_in >= b, moved[:, :128], jnp.zeros_like(moved[:, :128]))
            shifted_ref[slot, b * k:(b + 1) * k, 128:] = moved[:, 128:]
        spread = jnp.dot(weight_ref[v], shifted_ref[slot], preferred_element_type=jnp.float32)
        head = jnp.zeros((8, edge), jnp.float32)
        tail = jnp.zeros((8, width - edge), jnp.float32)
        for q in range(n_rows // 8):
            blk = spread[8 * q:8 * q + 8, :]
            moved = pltpu.roll(blk, 8 * SHIFTS * q, 1, stride=SHIFTS, stride_axis=0)
            head = head + jnp.where(lag >= 8 * SHIFTS * q, moved[:, :edge], 0.0)
            if width > edge:
                tail = tail + moved[:, edge:]
        for t in range(edge // 128):
            acc_ref[t, 8 * v:8 * v + 8, :] = head[:, 128 * t:128 * (t + 1)]
        for t in range((width - edge) // 128):
            acc_ref[edge // 128 + t, 8 * v:8 * v + 8, :] = tail[:, 128 * t:128 * (t + 1)]
    for t in range(width // 128):
        total = acc_ref[t, pl.ds(0, vb, stride=8), :]
        for s in range(1, 8):
            total = total + acc_ref[t, pl.ds(s, vb, stride=8), :]
        out_ref[:, 128 * t:128 * (t + 1)] = total


def convolve(picked, slip):
    v_local, k, width = picked.shape
    span = slip.shape[2]
    n_rows = -(-span // SHIFTS)
    n_rows = -(-n_rows // 8) * 8
    padded = jnp.pad(slip, ((0, 0), (0, 0), (0, n_rows * SHIFTS - span)))
    weight = padded.reshape(v_local, k, n_rows, SHIFTS).transpose(0, 2, 3, 1).reshape(v_local, n_rows, SHIFTS * k)
    vb = min(V_BLOCK, v_local)
    return pl.pallas_call(
        conv_kernel,
        grid=(v_local // vb,),
        in_specs=[
            pl.BlockSpec((vb, n_rows, SHIFTS * k), lambda i: (i, 0, 0)),
            pl.BlockSpec((vb, k, width), lambda i: (i, 0, 0)),
        ],
        out_specs=pl.BlockSpec((vb, width), lambda i: (i, 0)),
        out_shape=jax.ShapeDtypeStruct((v_local, width), jnp.float32),
        scratch_shapes=[pltpu.VMEM((3, SHIFTS * k, width), jnp.bfloat16), pltpu.VMEM((width // 128, 8 * vb, 128), jnp.float32)],
    )(weight, picked)


def body(sgt, taps, moment, index, slip):
    n_handler = lax.axis_size("handler")
    me = lax.axis_index("handler")
    local_t = sgt.shape[0]
    local_j = local_t // DEC
    n_taps = taps.shape[0]
    halo = (n_taps - 1 + DEC - 1) // DEC
    lowpass = lax.optimization_barrier(band_matrix(taps, local_t, local_j + halo))
    by_component = jnp.transpose(sgt, (1, 0, 2))
    tail = jnp.einsum("tj,ctp->cjp", lowpass[local_t - n_taps:, local_j:], by_component[:, local_t - n_taps:, :],
                      preferred_element_type=jnp.float32)
    carried = lax.ppermute(jnp.sum(moment[:, None, :] * tail, axis=0), "handler",
                           [(i, i + 1) for i in range(n_handler - 1)])
    filtered = jnp.einsum("tj,ctp->cjp", lowpass[:, :local_j], by_component, preferred_element_type=jnp.float32)
    own = jnp.sum(moment[:, None, :] * filtered, axis=0)
    own = own.at[:halo].add(carried)
    by_time = lax.all_gather(own.astype(jnp.bfloat16), "handler", axis=0, tiled=True)
    length = by_time.shape[1]
    v_local, k = index.shape
    flat_index = jnp.clip(index.reshape(-1), 0, length - 1)
    choose = (flat_index[:, None] == lax.broadcasted_iota(jnp.int32, (flat_index.shape[0], length), 1))
    rows = jnp.einsum("np,jp->nj", choose.astype(jnp.bfloat16), by_time, preferred_element_type=jnp.float32)
    picked = rows.astype(jnp.bfloat16).reshape(v_local, k, by_time.shape[0])
    return convolve(picked, slip)


def solution(mesh):
    in_specs = (
        P(("site", "handler"), None, None),
        P(),
        P(),
        P("handler", None),
        P("handler", None, None),
    )
    out_specs = P(("site", "handler"), None)
    return jax.shard_map(body, mesh=mesh, in_specs=in_specs, out_specs=out_specs, check_vma=False)
```
